32 devices in a mesh: ctx: 8 (over z, y), dp: 2 (over x), section: 2 (over core).
Axes of the slice: x: 2, y: 2, z: 4, core: 2. Of those that a mesh axis runs over, the one named last changes fastest.
Arguments:
- normed: bfloat16 [2, 3072, 1024], P('dp', 'ctx'), may hold values from -40 to 40
- w_query: bfloat16 [1024, 1024], P('dp', 'section'), may hold values from -0.1875 to 0.1875
- w_key: bfloat16 [1024, 1024], P('dp', 'section'), may hold values from -0.28125 to 0.28125
- w_value: bfloat16 [1024, 1024], P('dp', 'section'), may hold values from -0.1875 to 0.1875
- block_mask: int32 [24, 7], replicated, may hold values from 0 to 1, as said below
- cotangent: bfloat16 [2, 3072, 1024], P('dp', 'ctx', 'section'), may hold values from -8 to 8
Outputs:
- attended: bfloat16 [2, 3072, 1024], P('dp', 'ctx', 'section')
- grad_input: bfloat16 [2, 3072, 1024], P('dp', 'ctx')
- grad_weights: float32 [1024, 3, 1024], P(('ctx', 'dp'), None, 'section')
The draws below stay inside these ranges and needn't reach their ends.
Inputs may be any that keep to these rules, and one draw needn't show every extreme that they name: `block_mask`: every row has a 1 in column 3; no row names a key block outside 0 to 23; a row holds at most 5 ones, and some row holds exactly 5.
All inputs are finite; a program needn't handle non-finite values.
Results may differ from the reference program's by a relative error of at most 0.014.
The reference program's roundings to bfloat16 on the way count: a program that leaves them out, or rounds other values in their place, can miss the bound.
Values may be sent and summed in bfloat16 or wider, within the bound.
No kernel may reach another device: no remote copies, remote signals or barrier semaphores. Data moves between devices by JAX's collectives and lax.ppermute only.
A program may use at most 64 MiB of HBM per device.

```python
import jax
import jax.numpy as jnp
from jax import lax

D = 1024
HEADS = 16
HD = 64
BLOCK = 128
REACH = 3
LIVE = 5
BLOCKS_DEV = 3
SAMPLES = 2
SEQ = 3072
NBLK = 24
SPAN = 7
N_CTX = 8


def draw_normed(key, part):
    base_key, scale_key = jax.random.split(jax.random.fold_in(key, 11), 2)
    base = jnp.clip(jax.random.normal(base_key, (SAMPLES, SEQ, D), jnp.float32), -4.0, 4.0)
    row_scale = jnp.exp(jax.random.uniform(scale_key, (SAMPLES, SEQ, 1), jnp.float32, jnp.log(0.4), jnp.log(4.0)))
    return (base * row_scale).astype(jnp.bfloat16)


def query_key_pair(key):
    first_key, second_key = jax.random.split(jax.random.fold_in(key, 23))
    w_first = jnp.clip(jax.random.normal(first_key, (D, D), jnp.float32), -6.0, 6.0) * D ** (-0.5)
    w_second = jnp.clip(jax.random.normal(second_key, (D, D), jnp.float32), -6.0, 6.0) * D ** (-0.5)
    return (w_first, w_second)


def draw_w_query(key, part):
    return query_key_pair(key)[0].astype(jnp.bfloat16)


def draw_w_key(key, part):
    return query_key_pair(key)[1].astype(jnp.bfloat16)


def draw_block_mask(key, part):
    count_key, noise_key, force_key = jax.random.split(jax.random.fold_in(key, 37), 3)
    row_ids = jnp.arange(NBLK, dtype=jnp.int32)[:, None]
    columns = jnp.arange(SPAN, dtype=jnp.int32)[None, :]
    target = row_ids + columns - REACH
    inside = (target >= 0) & (target < NBLK)
    wanted = jax.random.randint(count_key, (NBLK, 1), 2, LIVE + 1)
    forced = (jax.random.randint(force_key, (NBLK, 1), 0, 3) == 0) | (row_ids == NBLK // 2)
    wanted = jnp.where(forced, LIVE, wanted)
    noise = jax.random.randint(noise_key, (NBLK, SPAN), 0, 4096)
    priority = noise * SPAN + columns
    priority = jnp.where(columns == REACH, 8192 * SPAN, priority)
    priority = jnp.where(inside, priority, -1 - columns)
    ranking = jnp.argsort(jnp.argsort(-priority, axis=1), axis=1)
    chosen = (ranking < wanted) & inside
    return chosen.astype(jnp.int32)


def levels(stream_key, extent, cuts, low, top_value):
    def one(dim, parts):
        heights = jax.random.uniform(jax.random.fold_in(jax.random.fold_in(stream_key, 6), dim), (parts,), jnp.float32, low / len(cuts), top_value / len(cuts))
        return jnp.repeat(jnp.exp(heights), extent[dim] // parts).reshape((-1,) + (1,) * (len(extent) - dim - 1))

    level = one(*cuts[0])
    for cut in cuts[1:]:
        level = level * one(*cut)
    return level


def normal_values(stream_key, dims, deviation, limit, cuts=(), held_as=jnp.bfloat16):
    values = deviation * jax.random.normal(stream_key, dims, jnp.float32)
    if cuts:
        values = values * levels(stream_key, dims, cuts, -0.22, 0.18)
    return jnp.clip(values, -limit, limit).astype(held_as)


def setup_inputs(seed: int = 0) -> dict:
    arg_keys = jax.random.split(jax.random.key(seed), 7)
    normed = draw_normed(jax.random.fold_in(arg_keys[6], 71), 0)
    w_query = draw_w_query(jax.random.fold_in(arg_keys[6], 71), 0)
    w_key = draw_w_key(jax.random.fold_in(arg_keys[6], 71), 0)
    w_value = normal_values(arg_keys[3], (D, D), D ** -0.5, 0.1875, ((0, 2), (1, 2)))
    block_mask = draw_block_mask(jax.random.fold_in(arg_keys[6], 71), 0)
    cotangent = normal_values(arg_keys[5], (SAMPLES, SEQ, D), 2.0, 8.0, ((0, 2), (1, 8), (2, 2)))
    return dict(normed=normed, w_query=w_query, w_key=w_key, w_value=w_value, block_mask=block_mask, cotangent=cotangent)


def attend(query_block, key_window, seen_slots):
    scores = jnp.einsum('qhd,skhd->hqsk', query_block.astype(jnp.float32), key_window.astype(jnp.float32)) * (HD ** -0.5)
    is_seen = seen_slots[None, None, :, None] > 0
    row_top = jnp.max(jnp.where(is_seen, scores, -jnp.inf), axis=(2, 3), keepdims=True)
    raised = jnp.where(is_seen, jnp.exp(scores - row_top), 0.0)
    return raised / jnp.sum(raised, axis=(2, 3), keepdims=True)


def one_sample(tokens, upstream, w_query, w_key, w_value, block_mask):
    queries = jnp.dot(tokens, w_query, preferred_element_type=jnp.float32).astype(jnp.bfloat16)
    key_rows = jnp.dot(tokens, w_key, preferred_element_type=jnp.float32).astype(jnp.bfloat16)
    value_rows = jnp.dot(tokens, w_value, preferred_element_type=jnp.float32).astype(jnp.bfloat16)
    span_len = 2 * REACH + 1
    score_scale = HD ** -0.5
    query_blocks = queries.reshape(NBLK, BLOCK, HEADS, HD)
    upstream_blocks = upstream.reshape(NBLK, BLOCK, HEADS, HD)
    padding = ((REACH, REACH), (0, 0), (0, 0), (0, 0))
    key_padded = jnp.pad(key_rows.reshape(NBLK, BLOCK, HEADS, HD), padding)
    value_padded = jnp.pad(value_rows.reshape(NBLK, BLOCK, HEADS, HD), padding)

    def step(running, block_at):
        key_acc, value_acc = running
        key_window = lax.dynamic_slice_in_dim(key_padded, block_at, span_len, 0)
        value_window = lax.dynamic_slice_in_dim(value_padded, block_at, span_len, 0)
        seen_slots = lax.dynamic_index_in_dim(block_mask, block_at, 0, False)
        query_block = lax.dynamic_index_in_dim(query_blocks, block_at, 0, False)
        upstream_block = lax.dynamic_index_in_dim(upstream_blocks, block_at, 0, False)
        probability = attend(query_block, key_window, seen_slots)
        weights = lax.optimization_barrier(probability.astype(jnp.bfloat16))
        mixed_out = jnp.einsum('hqsk,skhd->qhd', weights.astype(jnp.float32), value_window.astype(jnp.float32)).astype(jnp.bfloat16)
        prob_grad = jnp.einsum('qhd,skhd->hqsk', upstream_block.astype(jnp.float32), value_window.astype(jnp.float32))
        row_delta = jnp.sum(probability * prob_grad, axis=(2, 3), keepdims=True)
        score_grad = lax.optimization_barrier((probability * (prob_grad - row_delta)).astype(jnp.bfloat16))
        query_grad = (score_scale * jnp.einsum('hqsk,skhd->qhd', score_grad.astype(jnp.float32), key_window.astype(jnp.float32))).astype(jnp.bfloat16)
        key_part = score_scale * jnp.einsum('hqsk,qhd->skhd', score_grad.astype(jnp.float32), query_block.astype(jnp.float32))
        value_part = jnp.einsum('hqsk,qhd->skhd', weights.astype(jnp.float32), upstream_block.astype(jnp.float32))
        key_acc = lax.dynamic_update_slice_in_dim(key_acc, lax.dynamic_slice_in_dim(key_acc, block_at, span_len, 0) + key_part, block_at, 0)
        value_acc = lax.dynamic_update_slice_in_dim(value_acc, lax.dynamic_slice_in_dim(value_acc, block_at, span_len, 0) + value_part, block_at, 0)
        return (key_acc, value_acc), (mixed_out, query_grad)

    empty_grad = jnp.zeros((NBLK + 2 * REACH, BLOCK, HEADS, HD), jnp.float32)
    (key_acc, value_acc), (mixed_outs, query_grads) = lax.scan(step, (empty_grad, empty_grad), jnp.arange(NBLK, dtype=jnp.int32))
    attended = mixed_outs.reshape(SEQ, D)
    query_grad = query_grads.reshape(SEQ, D)
    key_grad = key_acc[REACH:REACH + NBLK].reshape(SEQ, D).astype(jnp.bfloat16)
    value_grad = value_acc[REACH:REACH + NBLK].reshape(SEQ, D).astype(jnp.bfloat16)
    grad_input = (jnp.dot(query_grad, w_query.T, preferred_element_type=jnp.float32)
                  + jnp.dot(key_grad, w_key.T, preferred_element_type=jnp.float32)
                  + jnp.dot(value_grad, w_value.T, preferred_element_type=jnp.float32)).astype(jnp.bfloat16)
    stacked = jnp.stack([query_grad, key_grad, value_grad], axis=1).reshape(N_CTX, BLOCKS_DEV * BLOCK, 3 * D)
    groups = tokens.reshape(N_CTX, BLOCKS_DEV * BLOCK, D)

    def add_group(running, group_pair):
        weight_term = jnp.dot(group_pair[0].T, group_pair[1], preferred_element_type=jnp.float32).astype(jnp.bfloat16)
        weight_term = lax.optimization_barrier(weight_term)
        return running + weight_term.astype(jnp.float32), None

    group_sum, _ = lax.scan(add_group, jnp.zeros((D, 3 * D), jnp.float32), (groups, stacked))
    return attended, grad_input, group_sum.reshape(D, 3, D)


def reference(normed, w_query, w_key, w_value, block_mask, cotangent):
    def per_sample(sample_pair):
        return one_sample(sample_pair[0], sample_pair[1], w_query, w_key, w_value, block_mask)

    attended, grad_input, sample_sums = lax.map(per_sample, (normed, cotangent))
    grad_weights = jnp.sum(sample_sums, axis=0) / SAMPLES
    return attended, grad_input, grad_weights
```

```python
import jax
import jax.numpy as jnp
from jax import lax
from jax.sharding import PartitionSpec as P

HD = 64
BLOCK = 128
REACH = 3


def shifted(value, axis, steps):
    count = lax.axis_size(axis)
    leading, last = (max(0, -steps), min(count, count - steps))
    return lax.ppermute(value, axis, [(source, source + steps) for source in range(leading, last)])


def head_major(rows, heads):
    return rows.reshape(rows.shape[0], heads, HD).transpose(1, 0, 2)


def token_major(cells):
    return cells.transpose(1, 0, 2).reshape(cells.shape[1], cells.shape[0] * cells.shape[2])


def section_sum(partial):
    count = lax.axis_size("section")
    if count != 2:
        return lax.psum(partial.astype(jnp.bfloat16), "section")
    mine = partial.astype(jnp.bfloat16)
    other = lax.ppermute(mine, "section", [(0, 1), (1, 0)])
    return (mine.astype(jnp.float32) + other.astype(jnp.float32)).astype(jnp.bfloat16)


def per_device(normed, w_query, w_key, w_value, block_mask, cotangent):
    tokens = normed[0]
    upstream = cotangent[0]
    length = tokens.shape[0]
    features = upstream.shape[1]
    heads = features // HD
    blocks = length // BLOCK
    span_len = 2 * REACH + 1
    halo = REACH * BLOCK
    score_scale = HD ** (-0.5)

    left_tokens = shifted(tokens[length - halo :], "ctx", 1)
    right_tokens = shifted(tokens[:halo], "ctx", -1)
    gathered = lax.all_gather(jnp.stack([w_query, w_key, w_value]), "dp", axis=1, tiled=True)
    query_full, key_full, value_full = gathered[0], gathered[1], gathered[2]

    queries = jnp.dot(tokens, query_full, preferred_element_type=jnp.float32).astype(jnp.bfloat16)
    frame_tokens = jnp.concatenate([left_tokens, tokens, right_tokens], axis=0)
    kv_weights = jnp.concatenate([key_full, value_full], axis=1)
    frame_kv = jnp.dot(frame_tokens, kv_weights, preferred_element_type=jnp.float32).astype(
        jnp.bfloat16
    )
    key_h = head_major(frame_kv[:, :features], heads)
    value_h = head_major(frame_kv[:, features:], heads)
    query_h = head_major(queries, heads)
    upstream_h = head_major(upstream, heads)

    first_block = lax.axis_index("ctx") * blocks
    own_mask = lax.dynamic_slice(block_mask, (first_block, 0), (blocks, span_len))

    outs, query_grads = [], []
    key_frame = None
    value_frame = None
    for i in range(blocks):
        query_block = query_h[:, i * BLOCK : (i + 1) * BLOCK]
        upstream_block = upstream_h[:, i * BLOCK : (i + 1) * BLOCK]
        key_window = key_h[:, i * BLOCK : (i + span_len) * BLOCK]
        value_window = value_h[:, i * BLOCK : (i + span_len) * BLOCK]
        seen = jnp.repeat(own_mask[i] > 0, BLOCK)[None, None, :]
        scores = (
            jnp.einsum("hqd,hkd->hqk", query_block, key_window, preferred_element_type=jnp.float32)
            * score_scale
        )
        row_top = jnp.max(jnp.where(seen, scores, -jnp.inf), axis=2, keepdims=True)
        raised = jnp.where(seen, jnp.exp(scores - row_top), 0.0)
        probability = raised / jnp.sum(raised, axis=2, keepdims=True)
        weights = probability.astype(jnp.bfloat16)
        outs.append(
            jnp.einsum("hqk,hkd->hqd", weights, value_window, preferred_element_type=jnp.float32)
        )
        prob_grad = jnp.einsum(
            "hqd,hkd->hqk", upstream_block, value_window, preferred_element_type=jnp.float32
        )
        row_delta = jnp.sum(probability * prob_grad, axis=2, keepdims=True)
        score_grad = (probability * (prob_grad - row_delta)).astype(jnp.bfloat16)
        query_grads.append(
            score_scale
            * jnp.einsum("hqk,hkd->hqd", score_grad, key_window, preferred_element_type=jnp.float32)
        )
        key_part = score_scale * jnp.einsum(
            "hqk,hqd->hkd", score_grad, query_block, preferred_element_type=jnp.float32
        )
        value_part = jnp.einsum(
            "hqk,hqd->hkd", weights, upstream_block, preferred_element_type=jnp.float32
        )
        spread = ((0, 0), (i * BLOCK, (blocks - 1 - i) * BLOCK), (0, 0))
        key_part = jnp.pad(key_part, spread)
        value_part = jnp.pad(value_part, spread)
        key_frame = key_part if key_frame is None else key_frame + key_part
        value_frame = value_part if value_frame is None else value_frame + value_part

    attended = token_major(jnp.concatenate(outs, axis=1).astype(jnp.bfloat16))[None]
    query_grad = token_major(jnp.concatenate(query_grads, axis=1).astype(jnp.bfloat16))

    frame_grads = jnp.stack([token_major(key_frame), token_major(value_frame)])
    to_left = frame_grads[:, :halo].astype(jnp.bfloat16)
    to_right = frame_grads[:, halo + length :].astype(jnp.bfloat16)
    middle = frame_grads[:, halo : halo + length]
    from_left = shifted(to_right, "ctx", 1).astype(jnp.float32)
    from_right = shifted(to_left, "ctx", -1).astype(jnp.float32)
    middle = middle.at[:, :halo].add(from_left)
    middle = middle.at[:, length - halo :].add(from_right)
    key_grad = middle[0].astype(jnp.bfloat16)
    value_grad = middle[1].astype(jnp.bfloat16)

    term_query = jnp.einsum(
        "tr,tf->rf", tokens, query_grad, preferred_element_type=jnp.float32
    ).astype(jnp.bfloat16)
    reduced_query = lax.psum_scatter(term_query, ("ctx", "dp"), scatter_dimension=0, tiled=True)

    contract = (((1,), (1,)), ((), ()))
    partial_input = (
        lax.dot_general(query_grad, query_full, contract, preferred_element_type=jnp.float32)
        + lax.dot_general(key_grad, key_full, contract, preferred_element_type=jnp.float32)
        + lax.dot_general(value_grad, value_full, contract, preferred_element_type=jnp.float32)
    )
    grad_input = section_sum(partial_input)[None]

    term_kv = jnp.einsum(
        "tr,tcf->rcf",
        tokens,
        jnp.stack([key_grad, value_grad], axis=1),
        preferred_element_type=jnp.float32,
    ).astype(jnp.bfloat16)
    reduced_kv = lax.psum_scatter(
        term_kv.reshape(term_kv.shape[0], 2 * features), ("ctx", "dp"), scatter_dimension=0, tiled=True
    ).reshape(-1, 2, features)
    summed = jnp.concatenate([reduced_query[:, None], reduced_kv], axis=1).astype(jnp.float32)
    grad_weights = summed / lax.axis_size("dp")
    return (attended, grad_input, grad_weights)


def solution(mesh):
    in_specs = (
        P("dp", "ctx", None),
        P("dp", "section"),
        P("dp", "section"),
        P("dp", "section"),
        P(),
        P("dp", "ctx", "section"),
    )
    out_specs = (P("dp", "ctx", "section"), P("dp", "ctx", None), P(("ctx", "dp"), None, "section"))
    return jax.shard_map(
        per_device, mesh=mesh, in_specs=in_specs, out_specs=out_specs, check_vma=False
    )
```

```python
import jax
import jax.numpy as jnp
from jax import lax
from jax.sharding import PartitionSpec as P

HD = 64
BLOCK = 128
REACH = 3


def shifted(value, axis, steps):
    count = lax.axis_size(axis)
    leading, last = (max(0, -steps), min(count, count - steps))
    return lax.ppermute(value, axis, [(source, source + steps) for source in range(leading, last)])


def head_major(rows, heads):
    return rows.reshape(rows.shape[0], heads, HD).transpose(1, 0, 2)


def token_major(cells):
    return cells.transpose(1, 0, 2).reshape(cells.shape[1], cells.shape[0] * cells.shape[2])


def ordered_pair(mine, other, axis, dim):
    first = lax.axis_index(axis) == 0
    return jnp.where(
        first,
        jnp.concatenate([mine, other], axis=dim),
        jnp.concatenate([other, mine], axis=dim),
    )


def neighbour_tokens(tokens, halo):
    count = lax.axis_size("section")
    if count != 2:
        return (shifted(tokens[-halo:], "ctx", 1), shifted(tokens[:halo], "ctx", -1))
    half = tokens.shape[1] // 2
    start = lax.axis_index("section") * half
    share = lax.dynamic_slice_in_dim(tokens, start, half, 1)
    fetched = jnp.stack([shifted(share[-halo:], "ctx", 1), shifted(share[:halo], "ctx", -1)])
    partner = lax.ppermute(fetched, "section", [(0, 1), (1, 0)])
    both = ordered_pair(fetched, partner, "section", 2)
    return (both[0], both[1])


def full_rows(weight):
    if lax.axis_size("dp") != 2:
        return lax.all_gather(weight, "dp", axis=0, tiled=True)
    other = lax.ppermute(weight, "dp", [(0, 1), (1, 0)])
    return ordered_pair(weight, other, "dp", 0)


def summed_rows(term):
    group = ("ctx", "dp")
    count = lax.axis_size(group)
    parts = lax.all_to_all(term, group, 0, 0, tiled=True)
    parts = parts.reshape(count, term.shape[0] // count, *term.shape[1:])
    return jnp.sum(parts.astype(jnp.float32), axis=0)


def section_sum(partial):
    count = lax.axis_size("section")
    if count != 2:
        return lax.psum(partial.astype(jnp.bfloat16), "section")
    mine = partial.astype(jnp.bfloat16)
    other = lax.ppermute(mine, "section", [(0, 1), (1, 0)])
    return (mine.astype(jnp.float32) + other.astype(jnp.float32)).astype(jnp.bfloat16)


def per_device(normed, w_query, w_key, w_value, block_mask, cotangent):
    tokens = normed[0]
    upstream = cotangent[0]
    length = tokens.shape[0]
    features = upstream.shape[1]
    heads = features // HD
    blocks = length // BLOCK
    span_len = 2 * REACH + 1
    halo = REACH * BLOCK
    score_scale = HD ** (-0.5)

    left_tokens, right_tokens = neighbour_tokens(tokens, halo)
    query_full = full_rows(w_query)
    gathered = lax.all_gather(jnp.stack([w_key, w_value]), "dp", axis=1, tiled=True)
    key_full, value_full = gathered[0], gathered[1]

    queries = jnp.dot(tokens, query_full, preferred_element_type=jnp.float32).astype(jnp.bfloat16)
    frame_tokens = jnp.concatenate([left_tokens, tokens, right_tokens], axis=0)
    kv_weights = jnp.concatenate([key_full, value_full], axis=1)
    frame_kv = jnp.dot(frame_tokens, kv_weights, preferred_element_type=jnp.float32).astype(
        jnp.bfloat16
    )
    key_h = head_major(frame_kv[:, :features], heads)
    value_h = head_major(frame_kv[:, features:], heads)
    query_h = head_major(queries, heads)
    upstream_h = head_major(upstream, heads)

    first_block = lax.axis_index("ctx") * blocks
    own_mask = lax.dynamic_slice(block_mask, (first_block, 0), (blocks, span_len))

    outs, query_grads = [], []
    key_frame = None
    value_frame = None
    for i in range(blocks):
        query_block = query_h[:, i * BLOCK : (i + 1) * BLOCK]
        upstream_block = upstream_h[:, i * BLOCK : (i + 1) * BLOCK]
        key_window = key_h[:, i * BLOCK : (i + span_len) * BLOCK]
        value_window = value_h[:, i * BLOCK : (i + span_len) * BLOCK]
        seen = jnp.repeat(own_mask[i] > 0, BLOCK)[None, None, :]
        scores = (
            jnp.einsum("hqd,hkd->hqk", query_block, key_window, preferred_element_type=jnp.float32)
            * score_scale
        )
        row_top = jnp.max(jnp.where(seen, scores, -jnp.inf), axis=2, keepdims=True)
        raised = jnp.where(seen, jnp.exp(scores - row_top), 0.0)
        probability = raised / jnp.sum(raised, axis=2, keepdims=True)
        weights = probability.astype(jnp.bfloat16)
        outs.append(
            jnp.einsum("hqk,hkd->hqd", weights, value_window, preferred_element_type=jnp.float32)
        )
        prob_grad = jnp.einsum(
            "hqd,hkd->hqk", upstream_block, value_window, preferred_element_type=jnp.float32
        )
        row_delta = jnp.sum(probability * prob_grad, axis=2, keepdims=True)
        score_grad = (probability * (prob_grad - row_delta)).astype(jnp.bfloat16)
        query_grads.append(
            score_scale
            * jnp.einsum("hqk,hkd->hqd", score_grad, key_window, preferred_element_type=jnp.float32)
        )
        key_part = score_scale * jnp.einsum(
            "hqk,hqd->hkd", score_grad, query_block, preferred_element_type=jnp.float32
        )
        value_part = jnp.einsum(
            "hqk,hqd->hkd", weights, upstream_block, preferred_element_type=jnp.float32
        )
        spread = ((0, 0), (i * BLOCK, (blocks - 1 - i) * BLOCK), (0, 0))
        key_part = jnp.pad(key_part, spread)
        value_part = jnp.pad(value_part, spread)
        key_frame = key_part if key_frame is None else key_frame + key_part
        value_frame = value_part if value_frame is None else value_frame + value_part

    attended = token_major(jnp.concatenate(outs, axis=1).astype(jnp.bfloat16))[None]
    query_grad = token_major(jnp.concatenate(query_grads, axis=1).astype(jnp.bfloat16))

    frame_grads = jnp.stack([token_major(key_frame), token_major(value_frame)])
    to_left = frame_grads[:, :halo].astype(jnp.bfloat16)
    to_right = frame_grads[:, halo + length :].astype(jnp.bfloat16)
    middle = frame_grads[:, halo : halo + length]
    from_left = shifted(to_right, "ctx", 1).astype(jnp.float32)
    from_right = shifted(to_left, "ctx", -1).astype(jnp.float32)
    middle = middle.at[:, :halo].add(from_left)
    middle = middle.at[:, length - halo :].add(from_right)
    key_grad = middle[0].astype(jnp.bfloat16)
    value_grad = middle[1].astype(jnp.bfloat16)

    term_query = jnp.einsum(
        "tr,tf->rf", tokens, query_grad, preferred_element_type=jnp.float32
    ).astype(jnp.bfloat16)
    reduced_query = lax.psum_scatter(term_query, ("ctx", "dp"), scatter_dimension=0, tiled=True)

    contract = (((1,), (1,)), ((), ()))
    partial_input = (
        lax.dot_general(query_grad, query_full, contract, preferred_element_type=jnp.float32)
        + lax.dot_general(key_grad, key_full, contract, preferred_element_type=jnp.float32)
        + lax.dot_general(value_grad, value_full, contract, preferred_element_type=jnp.float32)
    )
    grad_input = section_sum(partial_input)[None]

    term_kv = jnp.einsum(
        "tr,tcf->rcf",
        tokens,
        jnp.stack([key_grad, value_grad], axis=1),
        preferred_element_type=jnp.float32,
    ).astype(jnp.bfloat16)
    reduced_kv = summed_rows(term_kv)
    summed = jnp.concatenate([reduced_query[:, None].astype(jnp.float32), reduced_kv], axis=1)
    grad_weights = summed / lax.axis_size("dp")
    return (attended, grad_input, grad_weights)


def solution(mesh):
    in_specs = (
        P("dp", "ctx", None),
        P("dp", "section"),
        P("dp", "section"),
        P("dp", "section"),
        P(),
        P("dp", "ctx", "section"),
    )
    out_specs = (P("dp", "ctx", "section"), P("dp", "ctx", None), P(("ctx", "dp"), None, "section"))
    return jax.shard_map(
        per_device, mesh=mesh, in_specs=in_specs, out_specs=out_specs, check_vma=False
    )
```

```python
import jax
import jax.numpy as jnp
from jax import lax
from jax.sharding import PartitionSpec as P

HD = 64
BLOCK = 128
REACH = 3


def shifted(value, axis, steps):
    count = lax.axis_size(axis)
    leading, last = (max(0, -steps), min(count, count - steps))
    return lax.ppermute(value, axis, [(source, source + steps) for source in range(leading, last)])


def head_major(rows, heads):
    return rows.reshape(rows.shape[0], heads, HD).transpose(1, 0, 2)


def token_major(cells):
    return cells.transpose(1, 0, 2).reshape(cells.shape[1], cells.shape[0] * cells.shape[2])


def ordered_pair(mine, other, axis, dim):
    first = lax.axis_index(axis) == 0
    return jnp.where(
        first,
        jnp.concatenate([mine, other], axis=dim),
        jnp.concatenate([other, mine], axis=dim),
    )


def neighbour_tokens(tokens, halo):
    count = lax.axis_size("section")
    if count != 2:
        return (shifted(tokens[-halo:], "ctx", 1), shifted(tokens[:halo], "ctx", -1))
    half = tokens.shape[1] // 2
    start = lax.axis_index("section") * half
    share = lax.dynamic_slice_in_dim(tokens, start, half, 1)
    fetched = jnp.stack([shifted(share[-halo:], "ctx", 1), shifted(share[:halo], "ctx", -1)])
    partner = lax.ppermute(fetched, "section", [(0, 1), (1, 0)])
    both = ordered_pair(fetched, partner, "section", 2)
    return (both[0], both[1])


def full_rows(weight):
    if lax.axis_size("dp") != 2:
        return lax.all_gather(weight, "dp", axis=0, tiled=True)
    other = lax.ppermute(weight, "dp", [(0, 1), (1, 0)])
    return ordered_pair(weight, other, "dp", 0)


def summed_rows(term):
    group = ("ctx", "dp")
    count = lax.axis_size(group)
    parts = lax.all_to_all(term, group, 0, 0, tiled=True)
    parts = parts.reshape(count, term.shape[0] // count, *term.shape[1:])
    return jnp.sum(parts.astype(jnp.float32), axis=0)


def section_sum(partial):
    count = lax.axis_size("section")
    if count != 2:
        return lax.psum(partial.astype(jnp.bfloat16), "section")
    mine = partial.astype(jnp.bfloat16)
    other = lax.ppermute(mine, "section", [(0, 1), (1, 0)])
    return (mine.astype(jnp.float32) + other.astype(jnp.float32)).astype(jnp.bfloat16)


def per_device(normed, w_query, w_key, w_value, block_mask, cotangent):
    tokens = normed[0]
    upstream = cotangent[0]
    length = tokens.shape[0]
    features = upstream.shape[1]
    heads = features // HD
    blocks = length // BLOCK
    span_len = 2 * REACH + 1
    halo = REACH * BLOCK
    score_scale = HD ** (-0.5)

    left_tokens, right_tokens = neighbour_tokens(tokens, halo)
    query_full = full_rows(w_query)
    gathered = lax.all_gather(jnp.stack([w_key, w_value]), "dp", axis=1, tiled=True)
    key_full, value_full = gathered[0], gathered[1]

    queries = jnp.dot(tokens, query_full, preferred_element_type=jnp.float32).astype(jnp.bfloat16)
    frame_tokens = jnp.concatenate([left_tokens, tokens, right_tokens], axis=0)
    kv_weights = jnp.concatenate([key_full, value_full], axis=1)
    frame_kv = jnp.dot(frame_tokens, kv_weights, preferred_element_type=jnp.float32).astype(
        jnp.bfloat16
    )
    key_h = head_major(frame_kv[:, :features], heads)
    value_h = head_major(frame_kv[:, features:], heads)
    query_h = head_major(queries, heads)
    upstream_h = head_major(upstream, heads)

    first_block = lax.axis_index("ctx") * blocks
    own_mask = lax.dynamic_slice(block_mask, (first_block, 0), (blocks, span_len))

    outs, query_grads = [], []
    key_frame = None
    value_frame = None
    for i in range(blocks):
        query_block = query_h[:, i * BLOCK : (i + 1) * BLOCK]
        upstream_block = upstream_h[:, i * BLOCK : (i + 1) * BLOCK]
        key_window = key_h[:, i * BLOCK : (i + span_len) * BLOCK]
        value_window = value_h[:, i * BLOCK : (i + span_len) * BLOCK]
        seen = jnp.repeat(own_mask[i] > 0, BLOCK)[None, None, :]
        scores = (
            jnp.einsum("hqd,hkd->hqk", query_block, key_window, preferred_element_type=jnp.float32)
            * score_scale
        )
        row_top = jnp.max(jnp.where(seen, scores, -jnp.inf), axis=2, keepdims=True)
        raised = jnp.where(seen, jnp.exp(scores - row_top), 0.0)
        probability = raised / jnp.sum(raised, axis=2, keepdims=True)
        weights = probability.astype(jnp.bfloat16)
        outs.append(
            jnp.einsum("hqk,hkd->hqd", weights, value_window, preferred_element_type=jnp.float32)
        )
        prob_grad = jnp.einsum(
            "hqd,hkd->hqk", upstream_block, value_window, preferred_element_type=jnp.float32
        )
        row_delta = jnp.sum(probability * prob_grad, axis=2, keepdims=True)
        score_grad = (probability * (prob_grad - row_delta)).astype(jnp.bfloat16)
        query_grads.append(
            score_scale
            * jnp.einsum("hqk,hkd->hqd", score_grad, key_window, preferred_element_type=jnp.float32)
        )
        key_part = score_scale * jnp.einsum(
            "hqk,hqd->hkd", score_grad, query_block, preferred_element_type=jnp.float32
        )
        value_part = jnp.einsum(
            "hqk,hqd->hkd", weights, upstream_block, preferred_element_type=jnp.float32
        )
        spread = ((0, 0), (i * BLOCK, (blocks - 1 - i) * BLOCK), (0, 0))
        key_part = jnp.pad(key_part, spread)
        value_part = jnp.pad(value_part, spread)
        key_frame = key_part if key_frame is None else key_frame + key_part
        value_frame = value_part if value_frame is None else value_frame + value_part

    attended = token_major(jnp.concatenate(outs, axis=1).astype(jnp.bfloat16))[None]
    query_grad = token_major(jnp.concatenate(query_grads, axis=1).astype(jnp.bfloat16))

    frame_grads = jnp.stack([token_major(key_frame), token_major(value_frame)])
    to_left = frame_grads[:, :halo].astype(jnp.bfloat16)
    to_right = frame_grads[:, halo + length :].astype(jnp.bfloat16)
    middle = frame_grads[:, halo : halo + length]
    from_left = shifted(to_right, "ctx", 1).astype(jnp.float32)
    from_right = shifted(to_left, "ctx", -1).astype(jnp.float32)
    middle = middle.at[:, :halo].add(from_left)
    middle = middle.at[:, length - halo :].add(from_right)
    key_grad = middle[0].astype(jnp.bfloat16)
    value_grad = middle[1].astype(jnp.bfloat16)

    term_query = jnp.einsum(
        "tr,tf->rf", tokens, query_grad, preferred_element_type=jnp.float32
    ).astype(jnp.bfloat16)
    reduced_query = summed_rows(term_query)

    contract = (((1,), (1,)), ((), ()))
    partial_input = (
        lax.dot_general(query_grad, query_full, contract, preferred_element_type=jnp.float32)
        + lax.dot_general(key_grad, key_full, contract, preferred_element_type=jnp.float32)
        + lax.dot_general(value_grad, value_full, contract, preferred_element_type=jnp.float32)
    )
    grad_input = section_sum(partial_input)[None]

    term_kv = jnp.einsum(
        "tr,tcf->rcf",
        tokens,
        jnp.stack([key_grad, value_grad], axis=1),
        preferred_element_type=jnp.float32,
    ).astype(jnp.bfloat16)
    reduced_kv = summed_rows(term_kv)
    summed = jnp.concatenate([reduced_query[:, None], reduced_kv], axis=1)
    grad_weights = summed / lax.axis_size("dp")
    return (attended, grad_input, grad_weights)


def solution(mesh):
    in_specs = (
        P("dp", "ctx", None),
        P("dp", "section"),
        P("dp", "section"),
        P("dp", "section"),
        P(),
        P("dp", "ctx", "section"),
    )
    out_specs = (P("dp", "ctx", "section"), P("dp", "ctx", None), P(("ctx", "dp"), None, "section"))
    return jax.shard_map(
        per_device, mesh=mesh, in_specs=in_specs, out_specs=out_specs, check_vma=False
    )
```

```python
import jax
import jax.numpy as jnp
from jax import lax
from jax.sharding import PartitionSpec as P

HD = 64
BLOCK = 128
REACH = 3


def shifted(value, axis, steps):
    count = lax.axis_size(axis)
    leading, last = (max(0, -steps), min(count, count - steps))
    return lax.ppermute(value, axis, [(source, source + steps) for source in range(leading, last)])


def head_major(rows, heads):
    return rows.reshape(rows.shape[0], heads, HD).transpose(1, 0, 2)


def token_major(cells):
    return cells.transpose(1, 0, 2).reshape(cells.shape[1], cells.shape[0] * cells.shape[2])


def ordered_pair(mine, other, axis, dim):
    first = lax.axis_index(axis) == 0
    return jnp.where(
        first,
        jnp.concatenate([mine, other], axis=dim),
        jnp.concatenate([other, mine], axis=dim),
    )


def neighbour_tokens(tokens, halo):
    count = lax.axis_size("section")
    if count != 2:
        return (shifted(tokens[-halo:], "ctx", 1), shifted(tokens[:halo], "ctx", -1))
    half = tokens.shape[1] // 2
    start = lax.axis_index("section") * half
    share = lax.dynamic_slice_in_dim(tokens, start, half, 1)
    fetched = jnp.stack([shifted(share[-halo:], "ctx", 1), shifted(share[:halo], "ctx", -1)])
    partner = lax.ppermute(fetched, "section", [(0, 1), (1, 0)])
    both = ordered_pair(fetched, partner, "section", 2)
    return (both[0], both[1])


def full_rows(weight):
    if lax.axis_size("dp") != 2:
        return lax.all_gather(weight, "dp", axis=0, tiled=True)
    other = lax.ppermute(weight, "dp", [(0, 1), (1, 0)])
    return ordered_pair(weight, other, "dp", 0)


def summed_rows(term):
    group = ("ctx", "dp")
    count = lax.axis_size(group)
    parts = lax.all_to_all(term, group, 0, 0, tiled=True)
    parts = parts.reshape(count, term.shape[0] // count, *term.shape[1:])
    return jnp.sum(parts.astype(jnp.float32), axis=0)


def section_sum(partial):
    count = lax.axis_size("section")
    if count != 2:
        return lax.psum(partial.astype(jnp.bfloat16), "section")
    mine = partial.astype(jnp.bfloat16)
    other = lax.ppermute(mine, "section", [(0, 1), (1, 0)])
    return (mine.astype(jnp.float32) + other.astype(jnp.float32)).astype(jnp.bfloat16)


def softmax_stats(scores, seen):
    row_top = jnp.max(jnp.where(seen, scores, -jnp.inf), axis=2, keepdims=True)
    raised = jnp.where(seen, jnp.exp(scores - row_top), 0.0)
    row_total = jnp.sum(raised, axis=2, keepdims=True)
    return raised / row_total, row_top, row_total


def per_device(normed, w_query, w_key, w_value, block_mask, cotangent):
    tokens = normed[0]
    upstream = cotangent[0]
    length = tokens.shape[0]
    features = upstream.shape[1]
    heads = features // HD
    blocks = length // BLOCK
    span_len = 2 * REACH + 1
    halo = REACH * BLOCK
    frame_blocks = blocks + 2 * REACH
    score_scale = HD ** (-0.5)

    left_tokens, right_tokens = neighbour_tokens(tokens, halo)
    left_up = shifted(upstream[length - halo :], "ctx", 1)
    right_up = shifted(upstream[:halo], "ctx", -1)
    gathered = lax.all_gather(jnp.stack([w_query, w_key, w_value]), "dp", axis=1, tiled=True)
    query_full, key_full, value_full = gathered[0], gathered[1], gathered[2]

    frame_tokens = jnp.concatenate([left_tokens, tokens, right_tokens], axis=0)
    all_weights = jnp.concatenate([query_full, key_full, value_full], axis=1)
    frame_proj = jnp.dot(frame_tokens, all_weights, preferred_element_type=jnp.float32).astype(
        jnp.bfloat16
    )
    query_h = head_major(frame_proj[:, :features], heads)
    key_h = head_major(frame_proj[:, features : 2 * features], heads)
    value_h = head_major(frame_proj[:, 2 * features :], heads)
    upstream_h = head_major(jnp.concatenate([left_up, upstream, right_up], axis=0), heads)

    first_block = lax.axis_index("ctx") * blocks
    padded_mask = jnp.pad(block_mask, ((REACH, REACH), (0, 0)))
    frame_mask = lax.dynamic_slice(padded_mask, (first_block, 0), (frame_blocks, span_len))

    def rows(cells, at, count=1):
        return cells[:, at * BLOCK : (at + count) * BLOCK]

    def seen_keys(at, low, high):
        picked = frame_mask[at, low - at + REACH : high - at + REACH + 1] > 0
        return jnp.repeat(picked, BLOCK)[None, None, :]

    own_low, own_high = REACH, REACH + blocks - 1
    key_own = jnp.zeros((heads, length, HD), jnp.float32)
    value_own = jnp.zeros((heads, length, HD), jnp.float32)

    def add_own(acc, part, low, high):
        spread = ((0, 0), ((low - own_low) * BLOCK, (own_high - high) * BLOCK), (0, 0))
        return acc + jnp.pad(part, spread)

    outs, query_grads, tops, totals, deltas = [], [], [], [], []
    for i in range(blocks):
        at = REACH + i
        query_block = rows(query_h, at)
        upstream_block = rows(upstream_h, at)
        key_window = rows(key_h, i, span_len)
        value_window = rows(value_h, i, span_len)
        scores = (
            jnp.einsum("hqd,hkd->hqk", query_block, key_window, preferred_element_type=jnp.float32)
            * score_scale
        )
        probability, row_top, row_total = softmax_stats(scores, seen_keys(at, i, i + 2 * REACH))
        weights = probability.astype(jnp.bfloat16)
        outs.append(
            jnp.einsum("hqk,hkd->hqd", weights, value_window, preferred_element_type=jnp.float32)
        )
        prob_grad = jnp.einsum(
            "hqd,hkd->hqk", upstream_block, value_window, preferred_element_type=jnp.float32
        )
        row_delta = jnp.sum(probability * prob_grad, axis=2, keepdims=True)
        score_grad = (probability * (prob_grad - row_delta)).astype(jnp.bfloat16)
        query_grads.append(
            score_scale
            * jnp.einsum("hqk,hkd->hqd", score_grad, key_window, preferred_element_type=jnp.float32)
        )
        tops.append(row_top)
        totals.append(row_total)
        deltas.append(row_delta)
        low, high = max(own_low, i), min(own_high, i + 2 * REACH)
        cut = slice((low - i) * BLOCK, (high - i + 1) * BLOCK)
        key_own = add_own(
            key_own,
            score_scale
            * jnp.einsum(
                "hqk,hqd->hkd", score_grad[:, :, cut], query_block, preferred_element_type=jnp.float32
            ),
            low,
            high,
        )
        value_own = add_own(
            value_own,
            jnp.einsum(
                "hqk,hqd->hkd", weights[:, :, cut], upstream_block, preferred_element_type=jnp.float32
            ),
            low,
            high,
        )

    attended = token_major(jnp.concatenate(outs, axis=1).astype(jnp.bfloat16))[None]
    query_grad = token_major(jnp.concatenate(query_grads, axis=1).astype(jnp.bfloat16))

    term_query = jnp.einsum(
        "tr,tf->rf", tokens, query_grad, preferred_element_type=jnp.float32
    ).astype(jnp.bfloat16)
    reduced_query = summed_rows(term_query)

    stats = jnp.stack(
        [jnp.concatenate(tops, axis=1), jnp.concatenate(totals, axis=1), jnp.concatenate(deltas, axis=1)]
    )
    stats_left = shifted(stats[:, :, length - halo :], "ctx", 1)
    stats_right = shifted(stats[:, :, :halo], "ctx", -1)

    for at in list(range(REACH)) + list(range(REACH + blocks, frame_blocks)):
        low, high = max(own_low, at - REACH), min(own_high, at + REACH)
        if low > high:
            continue
        if at < REACH:
            top, total, delta = (part[:, at * BLOCK : (at + 1) * BLOCK] for part in stats_left)
        else:
            place = at - REACH - blocks
            top, total, delta = (part[:, place * BLOCK : (place + 1) * BLOCK] for part in stats_right)
        query_block = rows(query_h, at)
        upstream_block = rows(upstream_h, at)
        key_part = rows(key_h, low, high - low + 1)
        value_part = rows(value_h, low, high - low + 1)
        seen = seen_keys(at, low, high)
        scores = (
            jnp.einsum("hqd,hkd->hqk", query_block, key_part, preferred_element_type=jnp.float32)
            * score_scale
        )
        probability = jnp.where(seen, jnp.exp(scores - top) / total, 0.0)
        weights = probability.astype(jnp.bfloat16)
        prob_grad = jnp.einsum(
            "hqd,hkd->hqk", upstream_block, value_part, preferred_element_type=jnp.float32
        )
        score_grad = (probability * (prob_grad - delta)).astype(jnp.bfloat16)
        key_own = add_own(
            key_own,
            score_scale
            * jnp.einsum("hqk,hqd->hkd", score_grad, query_block, preferred_element_type=jnp.float32),
            low,
            high,
        )
        value_own = add_own(
            value_own,
            jnp.einsum("hqk,hqd->hkd", weights, upstream_block, preferred_element_type=jnp.float32),
            low,
            high,
        )

    key_grad = token_major(key_own).astype(jnp.bfloat16)
    value_grad = token_major(value_own).astype(jnp.bfloat16)

    contract = (((1,), (1,)), ((), ()))
    partial_input = (
        lax.dot_general(query_grad, query_full, contract, preferred_element_type=jnp.float32)
        + lax.dot_general(key_grad, key_full, contract, preferred_element_type=jnp.float32)
        + lax.dot_general(value_grad, value_full, contract, preferred_element_type=jnp.float32)
    )
    grad_input = section_sum(partial_input)[None]

    term_kv = jnp.einsum(
        "tr,tcf->rcf",
        tokens,
        jnp.stack([key_grad, value_grad], axis=1),
        preferred_element_type=jnp.float32,
    ).astype(jnp.bfloat16)
    reduced_kv = summed_rows(term_kv)
    summed = jnp.concatenate([reduced_query[:, None], reduced_kv], axis=1)
    grad_weights = summed / lax.axis_size("dp")
    return (attended, grad_input, grad_weights)


def solution(mesh):
    in_specs = (
        P("dp", "ctx", None),
        P("dp", "section"),
        P("dp", "section"),
        P("dp", "section"),
        P(),
        P("dp", "ctx", "section"),
    )
    out_specs = (P("dp", "ctx", "section"), P("dp", "ctx", None), P(("ctx", "dp"), None, "section"))
    return jax.shard_map(
        per_device, mesh=mesh, in_specs=in_specs, out_specs=out_specs, check_vma=False
    )
```

```python
import jax
import jax.numpy as jnp
from jax import lax
from jax.sharding import PartitionSpec as P

HD = 64
BLOCK = 128
REACH = 3


def shifted(value, axis, steps):
    count = lax.axis_size(axis)
    leading, last = (max(0, -steps), min(count, count - steps))
    return lax.ppermute(value, axis, [(source, source + steps) for source in range(leading, last)])


def head_major(rows, heads):
    return rows.reshape(rows.shape[0], heads, HD).transpose(1, 0, 2)


def token_major(cells):
    return cells.transpose(1, 0, 2).reshape(cells.shape[1], cells.shape[0] * cells.shape[2])


def ordered_pair(mine, other, axis, dim):
    first = lax.axis_index(axis) == 0
    return jnp.where(
        first,
        jnp.concatenate([mine, other], axis=dim),
        jnp.concatenate([other, mine], axis=dim),
    )


def neighbour_tokens(tokens, halo):
    count = lax.axis_size("section")
    if count != 2:
        return (shifted(tokens[-halo:], "ctx", 1), shifted(tokens[:halo], "ctx", -1))
    half = tokens.shape[1] // 2
    start = lax.axis_index("section") * half
    share = lax.dynamic_slice_in_dim(tokens, start, half, 1)
    fetched = jnp.stack([shifted(share[-halo:], "ctx", 1), shifted(share[:halo], "ctx", -1)])
    partner = lax.ppermute(fetched, "section", [(0, 1), (1, 0)])
    both = ordered_pair(fetched, partner, "section", 2)
    return (both[0], both[1])


def full_rows(weight):
    if lax.axis_size("dp") != 2:
        return lax.all_gather(weight, "dp", axis=0, tiled=True)
    other = lax.ppermute(weight, "dp", [(0, 1), (1, 0)])
    return ordered_pair(weight, other, "dp", 0)


def summed_rows(term):
    group = ("ctx", "dp")
    count = lax.axis_size(group)
    parts = lax.all_to_all(term, group, 0, 0, tiled=True)
    parts = parts.reshape(count, term.shape[0] // count, *term.shape[1:])
    return jnp.sum(parts.astype(jnp.float32), axis=0)


def section_sum(partial):
    count = lax.axis_size("section")
    if count != 2:
        return lax.psum(partial.astype(jnp.bfloat16), "section")
    mine = partial.astype(jnp.bfloat16)
    other = lax.ppermute(mine, "section", [(0, 1), (1, 0)])
    return (mine.astype(jnp.float32) + other.astype(jnp.float32)).astype(jnp.bfloat16)


def softmax_stats(scores, seen):
    row_top = jnp.max(jnp.where(seen, scores, -jnp.inf), axis=2, keepdims=True)
    raised = jnp.where(seen, jnp.exp(scores - row_top), 0.0)
    row_total = jnp.sum(raised, axis=2, keepdims=True)
    return raised / row_total, row_top, row_total


def per_device(normed, w_query, w_key, w_value, block_mask, cotangent):
    tokens = normed[0]
    upstream = cotangent[0]
    length = tokens.shape[0]
    features = upstream.shape[1]
    heads = features // HD
    blocks = length // BLOCK
    span_len = 2 * REACH + 1
    halo = REACH * BLOCK
    frame_blocks = blocks + 2 * REACH
    score_scale = HD ** (-0.5)

    left_tokens, right_tokens = neighbour_tokens(tokens, halo)
    left_up = shifted(upstream[length - halo :], "ctx", 1)
    right_up = shifted(upstream[:halo], "ctx", -1)
    gathered = lax.all_gather(jnp.stack([w_query, w_key, w_value]), "dp", axis=1, tiled=True)
    query_full, key_full, value_full = gathered[0], gathered[1], gathered[2]

    frame_tokens = jnp.concatenate([left_tokens, tokens, right_tokens], axis=0)
    all_weights = jnp.concatenate([query_full, key_full, value_full], axis=1)
    frame_proj = jnp.dot(frame_tokens, all_weights, preferred_element_type=jnp.float32).astype(
        jnp.bfloat16
    )
    query_h = head_major(frame_proj[:, :features], heads)
    key_h = head_major(frame_proj[:, features : 2 * features], heads)
    value_h = head_major(frame_proj[:, 2 * features :], heads)
    upstream_h = head_major(jnp.concatenate([left_up, upstream, right_up], axis=0), heads)

    first_block = lax.axis_index("ctx") * blocks
    padded_mask = jnp.pad(block_mask, ((REACH, REACH), (0, 0)))
    frame_mask = lax.dynamic_slice(padded_mask, (first_block, 0), (frame_blocks, span_len))

    def rows(cells, at, count=1):
        return cells[:, at * BLOCK : (at + count) * BLOCK]

    def seen_keys(at, low, high):
        picked = frame_mask[at, low - at + REACH : high - at + REACH + 1] > 0
        return jnp.repeat(picked, BLOCK)[None, None, :]

    own_low, own_high = REACH, REACH + blocks - 1
    outs, query_grads, tops, totals, deltas = [], [], [], [], []
    own_score_grads, own_weights = [], []
    for i in range(blocks):
        at = REACH + i
        query_block = rows(query_h, at)
        upstream_block = rows(upstream_h, at)
        key_window = rows(key_h, i, span_len)
        value_window = rows(value_h, i, span_len)
        scores = (
            jnp.einsum("hqd,hkd->hqk", query_block, key_window, preferred_element_type=jnp.float32)
            * score_scale
        )
        probability, row_top, row_total = softmax_stats(scores, seen_keys(at, i, i + 2 * REACH))
        weights = probability.astype(jnp.bfloat16)
        outs.append(
            jnp.einsum("hqk,hkd->hqd", weights, value_window, preferred_element_type=jnp.float32)
        )
        prob_grad = jnp.einsum(
            "hqd,hkd->hqk", upstream_block, value_window, preferred_element_type=jnp.float32
        )
        row_delta = jnp.sum(probability * prob_grad, axis=2, keepdims=True)
        score_grad = (probability * (prob_grad - row_delta)).astype(jnp.bfloat16)
        query_grads.append(
            score_scale
            * jnp.einsum("hqk,hkd->hqd", score_grad, key_window, preferred_element_type=jnp.float32)
        )
        tops.append(row_top)
        totals.append(row_total)
        deltas.append(row_delta)
        cut = slice((own_low - i) * BLOCK, (own_high - i + 1) * BLOCK)
        own_score_grads.append(score_grad[:, :, cut])
        own_weights.append(weights[:, :, cut])

    attended = token_major(jnp.concatenate(outs, axis=1).astype(jnp.bfloat16))[None]
    query_grad = token_major(jnp.concatenate(query_grads, axis=1).astype(jnp.bfloat16))

    term_query = jnp.einsum(
        "tr,tf->rf", tokens, query_grad, preferred_element_type=jnp.float32
    ).astype(jnp.bfloat16)
    reduced_query = summed_rows(term_query)

    stats = jnp.stack(
        [jnp.concatenate(tops, axis=1), jnp.concatenate(totals, axis=1), jnp.concatenate(deltas, axis=1)]
    )
    stats_left = shifted(stats[:, :, length - halo :], "ctx", 1)
    stats_right = shifted(stats[:, :, :halo], "ctx", -1)

    near = list(range(REACH)) + list(range(REACH + blocks, frame_blocks))
    allowed = []
    for at in near:
        row = []
        for block in range(own_low, own_high + 1):
            slot = block - at + REACH
            row.append(frame_mask[at, slot] > 0 if 0 <= slot < span_len else jnp.zeros((), bool))
        allowed.append(jnp.stack(row))
    allowed = jnp.repeat(jnp.repeat(jnp.stack(allowed), BLOCK, axis=0), BLOCK, axis=1)[None]
    near_stats = jnp.concatenate([stats_left, stats_right], axis=2)
    top, total, delta = near_stats[0], near_stats[1], near_stats[2]
    near_query = jnp.concatenate([rows(query_h, 0, REACH), rows(query_h, REACH + blocks, REACH)], axis=1)
    near_upstream = jnp.concatenate(
        [rows(upstream_h, 0, REACH), rows(upstream_h, REACH + blocks, REACH)], axis=1
    )
    key_part = rows(key_h, own_low, blocks)
    value_part = rows(value_h, own_low, blocks)
    scores = (
        jnp.einsum("hqd,hkd->hqk", near_query, key_part, preferred_element_type=jnp.float32)
        * score_scale
    )
    probability = jnp.where(allowed, jnp.exp(scores - top) / total, 0.0)
    weights = probability.astype(jnp.bfloat16)
    prob_grad = jnp.einsum(
        "hqd,hkd->hqk", near_upstream, value_part, preferred_element_type=jnp.float32
    )
    score_grad = (probability * (prob_grad - delta)).astype(jnp.bfloat16)
    all_score_grads = jnp.concatenate(own_score_grads + [score_grad], axis=1)
    all_weights = jnp.concatenate(own_weights + [weights], axis=1)
    all_queries = jnp.concatenate([rows(query_h, REACH, blocks), near_query], axis=1)
    all_upstream = jnp.concatenate([rows(upstream_h, REACH, blocks), near_upstream], axis=1)
    key_own = score_scale * jnp.einsum(
        "hqk,hqd->hkd", all_score_grads, all_queries, preferred_element_type=jnp.float32
    )
    value_own = jnp.einsum(
        "hqk,hqd->hkd", all_weights, all_upstream, preferred_element_type=jnp.float32
    )

    key_grad = token_major(key_own).astype(jnp.bfloat16)
    value_grad = token_major(value_own).astype(jnp.bfloat16)

    contract = (((1,), (1,)), ((), ()))
    partial_input = (
        lax.dot_general(query_grad, query_full, contract, preferred_element_type=jnp.float32)
        + lax.dot_general(key_grad, key_full, contract, preferred_element_type=jnp.float32)
        + lax.dot_general(value_grad, value_full, contract, preferred_element_type=jnp.float32)
    )
    grad_input = section_sum(partial_input)[None]

    term_kv = jnp.einsum(
        "tr,tcf->rcf",
        tokens,
        jnp.stack([key_grad, value_grad], axis=1),
        preferred_element_type=jnp.float32,
    ).astype(jnp.bfloat16)
    reduced_kv = summed_rows(term_kv)
    summed = jnp.concatenate([reduced_query[:, None], reduced_kv], axis=1)
    grad_weights = summed / lax.axis_size("dp")
    return (attended, grad_input, grad_weights)


def solution(mesh):
    in_specs = (
        P("dp", "ctx", None),
        P("dp", "section"),
        P("dp", "section"),
        P("dp", "section"),
        P(),
        P("dp", "ctx", "section"),
    )
    out_specs = (P("dp", "ctx", "section"), P("dp", "ctx", None), P(("ctx", "dp"), None, "section"))
    return jax.shard_map(
        per_device, mesh=mesh, in_specs=in_specs, out_specs=out_specs, check_vma=False
    )
```

```python
import jax
import jax.numpy as jnp
from jax import lax
from jax.sharding import PartitionSpec as P

HD = 64
BLOCK = 128
REACH = 3


def shifted(value, axis, steps):
    count = lax.axis_size(axis)
    leading, last = (max(0, -steps), min(count, count - steps))
    return lax.ppermute(value, axis, [(source, source + steps) for source in range(leading, last)])


def head_major(rows, heads):
    return rows.reshape(rows.shape[0], heads, HD).transpose(1, 0, 2)


def token_major(cells):
    return cells.transpose(1, 0, 2).reshape(cells.shape[1], cells.shape[0] * cells.shape[2])


def ordered_pair(mine, other, axis, dim):
    first = lax.axis_index(axis) == 0
    return jnp.where(
        first,
        jnp.concatenate([mine, other], axis=dim),
        jnp.concatenate([other, mine], axis=dim),
    )


def neighbour_tokens(tokens, halo):
    count = lax.axis_size("section")
    if count != 2:
        return (shifted(tokens[-halo:], "ctx", 1), shifted(tokens[:halo], "ctx", -1))
    half = tokens.shape[1] // 2
    start = lax.axis_index("section") * half
    share = lax.dynamic_slice_in_dim(tokens, start, half, 1)
    fetched = jnp.stack([shifted(share[-halo:], "ctx", 1), shifted(share[:halo], "ctx", -1)])
    partner = lax.ppermute(fetched, "section", [(0, 1), (1, 0)])
    both = ordered_pair(fetched, partner, "section", 2)
    return (both[0], both[1])


def full_rows(weight):
    if lax.axis_size("dp") != 2:
        return lax.all_gather(weight, "dp", axis=0, tiled=True)
    other = lax.ppermute(weight, "dp", [(0, 1), (1, 0)])
    return ordered_pair(weight, other, "dp", 0)


def summed_rows(term):
    group = ("ctx", "dp")
    count = lax.axis_size(group)
    parts = lax.all_to_all(term, group, 0, 0, tiled=True)
    parts = parts.reshape(count, term.shape[0] // count, *term.shape[1:])
    return jnp.sum(parts.astype(jnp.float32), axis=0)


def section_sum(partial):
    count = lax.axis_size("section")
    if count != 2:
        return lax.psum(partial.astype(jnp.bfloat16), "section")
    mine = partial.astype(jnp.bfloat16)
    other = lax.ppermute(mine, "section", [(0, 1), (1, 0)])
    return (mine.astype(jnp.float32) + other.astype(jnp.float32)).astype(jnp.bfloat16)


def softmax_stats(scores, seen):
    row_top = jnp.max(jnp.where(seen, scores, -jnp.inf), axis=2, keepdims=True)
    raised = jnp.where(seen, jnp.exp(scores - row_top), 0.0)
    row_total = jnp.sum(raised, axis=2, keepdims=True)
    return raised / row_total, row_top, row_total


def per_device(normed, w_query, w_key, w_value, block_mask, cotangent):
    tokens = normed[0]
    upstream = cotangent[0]
    length = tokens.shape[0]
    features = upstream.shape[1]
    heads = features // HD
    blocks = length // BLOCK
    span_len = 2 * REACH + 1
    halo = REACH * BLOCK
    frame_blocks = blocks + 2 * REACH
    score_scale = HD ** (-0.5)

    left_tokens, right_tokens = neighbour_tokens(tokens, halo)
    query_full = full_rows(w_query)
    gathered = lax.all_gather(jnp.stack([w_key, w_value]), "dp", axis=1, tiled=True)
    key_full, value_full = gathered[0], gathered[1]

    frame_tokens = jnp.concatenate([left_tokens, tokens, right_tokens], axis=0)
    all_weights = jnp.concatenate([query_full, key_full, value_full], axis=1)
    frame_proj = jnp.dot(frame_tokens, all_weights, preferred_element_type=jnp.float32).astype(
        jnp.bfloat16
    )
    frame_proj, up_head, up_tail = lax.optimization_barrier(
        (frame_proj, upstream[:halo], upstream[length - halo :])
    )
    left_up = shifted(up_tail, "ctx", 1)
    right_up = shifted(up_head, "ctx", -1)
    query_h = head_major(frame_proj[:, :features], heads)
    key_h = head_major(frame_proj[:, features : 2 * features], heads)
    value_h = head_major(frame_proj[:, 2 * features :], heads)
    upstream_h = head_major(jnp.concatenate([left_up, upstream, right_up], axis=0), heads)

    first_block = lax.axis_index("ctx") * blocks
    padded_mask = jnp.pad(block_mask, ((REACH, REACH), (0, 0)))
    frame_mask = lax.dynamic_slice(padded_mask, (first_block, 0), (frame_blocks, span_len))

    def rows(cells, at, count=1):
        return cells[:, at * BLOCK : (at + count) * BLOCK]

    def seen_keys(at, low, high):
        picked = frame_mask[at, low - at + REACH : high - at + REACH + 1] > 0
        return jnp.repeat(picked, BLOCK)[None, None, :]

    own_low, own_high = REACH, REACH + blocks - 1
    outs, query_grads, tops, totals, deltas = [], [], [], [], []
    own_score_grads, own_weights = [], []
    for i in range(blocks):
        at = REACH + i
        query_block = rows(query_h, at)
        upstream_block = rows(upstream_h, at)
        key_window = rows(key_h, i, span_len)
        value_window = rows(value_h, i, span_len)
        scores = (
            jnp.einsum("hqd,hkd->hqk", query_block, key_window, preferred_element_type=jnp.float32)
            * score_scale
        )
        probability, row_top, row_total = softmax_stats(scores, seen_keys(at, i, i + 2 * REACH))
        weights = probability.astype(jnp.bfloat16)
        outs.append(
            jnp.einsum("hqk,hkd->hqd", weights, value_window, preferred_element_type=jnp.float32)
        )
        prob_grad = jnp.einsum(
            "hqd,hkd->hqk", upstream_block, value_window, preferred_element_type=jnp.float32
        )
        row_delta = jnp.sum(probability * prob_grad, axis=2, keepdims=True)
        score_grad = (probability * (prob_grad - row_delta)).astype(jnp.bfloat16)
        query_grads.append(
            score_scale
            * jnp.einsum("hqk,hkd->hqd", score_grad, key_window, preferred_element_type=jnp.float32)
        )
        tops.append(row_top)
        totals.append(row_total)
        deltas.append(row_delta)
        cut = slice((own_low - i) * BLOCK, (own_high - i + 1) * BLOCK)
        own_score_grads.append(score_grad[:, :, cut])
        own_weights.append(weights[:, :, cut])

    attended = token_major(jnp.concatenate(outs, axis=1).astype(jnp.bfloat16))[None]
    query_grad = token_major(jnp.concatenate(query_grads, axis=1).astype(jnp.bfloat16))

    term_query = jnp.einsum(
        "tr,tf->rf", tokens, query_grad, preferred_element_type=jnp.float32
    ).astype(jnp.bfloat16)
    reduced_query = summed_rows(term_query)

    stats = jnp.stack(
        [jnp.concatenate(tops, axis=1), jnp.concatenate(totals, axis=1), jnp.concatenate(deltas, axis=1)]
    )
    stats_left = shifted(stats[:, :, length - halo :], "ctx", 1)
    stats_right = shifted(stats[:, :, :halo], "ctx", -1)

    near = list(range(REACH)) + list(range(REACH + blocks, frame_blocks))
    allowed = []
    for at in near:
        row = []
        for block in range(own_low, own_high + 1):
            slot = block - at + REACH
            row.append(frame_mask[at, slot] > 0 if 0 <= slot < span_len else jnp.zeros((), bool))
        allowed.append(jnp.stack(row))
    allowed = jnp.repeat(jnp.repeat(jnp.stack(allowed), BLOCK, axis=0), BLOCK, axis=1)[None]
    near_stats = jnp.concatenate([stats_left, stats_right], axis=2)
    top, total, delta = near_stats[0], near_stats[1], near_stats[2]
    near_query = jnp.concatenate([rows(query_h, 0, REACH), rows(query_h, REACH + blocks, REACH)], axis=1)
    near_upstream = jnp.concatenate(
        [rows(upstream_h, 0, REACH), rows(upstream_h, REACH + blocks, REACH)], axis=1
    )
    key_part = rows(key_h, own_low, blocks)
    value_part = rows(value_h, own_low, blocks)
    scores = (
        jnp.einsum("hqd,hkd->hqk", near_query, key_part, preferred_element_type=jnp.float32)
        * score_scale
    )
    probability = jnp.where(allowed, jnp.exp(scores - top) / total, 0.0)
    weights = probability.astype(jnp.bfloat16)
    prob_grad = jnp.einsum(
        "hqd,hkd->hqk", near_upstream, value_part, preferred_element_type=jnp.float32
    )
    score_grad = (probability * (prob_grad - delta)).astype(jnp.bfloat16)
    all_score_grads = jnp.concatenate(own_score_grads + [score_grad], axis=1)
    all_weights = jnp.concatenate(own_weights + [weights], axis=1)
    all_queries = jnp.concatenate([rows(query_h, REACH, blocks), near_query], axis=1)
    all_upstream = jnp.concatenate([rows(upstream_h, REACH, blocks), near_upstream], axis=1)
    key_own = score_scale * jnp.einsum(
        "hqk,hqd->hkd", all_score_grads, all_queries, preferred_element_type=jnp.float32
    )
    value_own = jnp.einsum(
        "hqk,hqd->hkd", all_weights, all_upstream, preferred_element_type=jnp.float32
    )

    key_grad = token_major(key_own).astype(jnp.bfloat16)
    value_grad = token_major(value_own).astype(jnp.bfloat16)

    contract = (((1,), (1,)), ((), ()))
    partial_input = (
        lax.dot_general(query_grad, query_full, contract, preferred_element_type=jnp.float32)
        + lax.dot_general(key_grad, key_full, contract, preferred_element_type=jnp.float32)
        + lax.dot_general(value_grad, value_full, contract, preferred_element_type=jnp.float32)
    )
    grad_input = section_sum(partial_input)[None]

    term_kv = jnp.einsum(
        "tr,tf->rf",
        tokens,
        jnp.concatenate([key_grad, value_grad], axis=1),
        preferred_element_type=jnp.float32,
    ).astype(jnp.bfloat16)
    reduced_kv = summed_rows(term_kv).reshape(-1, 2, features)
    summed = jnp.concatenate([reduced_query[:, None], reduced_kv], axis=1)
    grad_weights = summed / lax.axis_size("dp")
    return (attended, grad_input, grad_weights)


def solution(mesh):
    in_specs = (
        P("dp", "ctx", None),
        P("dp", "section"),
        P("dp", "section"),
        P("dp", "section"),
        P(),
        P("dp", "ctx", "section"),
    )
    out_specs = (P("dp", "ctx", "section"), P("dp", "ctx", None), P(("ctx", "dp"), None, "section"))
    return jax.shard_map(
        per_device, mesh=mesh, in_specs=in_specs, out_specs=out_specs, check_vma=False
    )
```

```python
import jax
import jax.numpy as jnp
from jax import lax
from jax.sharding import PartitionSpec as P

HD = 64
BLOCK = 128
REACH = 3


def shifted(value, axis, steps):
    count = lax.axis_size(axis)
    leading, last = (max(0, -steps), min(count, count - steps))
    return lax.ppermute(value, axis, [(source, source + steps) for source in range(leading, last)])


def head_major(rows, heads):
    return rows.reshape(rows.shape[0], heads, HD).transpose(1, 0, 2)


def token_major(cells):
    return cells.transpose(1, 0, 2).reshape(cells.shape[1], cells.shape[0] * cells.shape[2])


def ordered_pair(mine, other, axis, dim):
    first = lax.axis_index(axis) == 0
    return jnp.where(
        first,
        jnp.concatenate([mine, other], axis=dim),
        jnp.concatenate([other, mine], axis=dim),
    )


def neighbour_tokens(tokens, halo):
    count = lax.axis_size("section")
    if count != 2:
        return (shifted(tokens[-halo:], "ctx", 1), shifted(tokens[:halo], "ctx", -1))
    half = tokens.shape[1] // 2
    start = lax.axis_index("section") * half
    share = lax.dynamic_slice_in_dim(tokens, start, half, 1)
    fetched = jnp.stack([shifted(share[-halo:], "ctx", 1), shifted(share[:halo], "ctx", -1)])
    partner = lax.ppermute(fetched, "section", [(0, 1), (1, 0)])
    both = ordered_pair(fetched, partner, "section", 2)
    return (both[0], both[1])


def full_rows(weight):
    if lax.axis_size("dp") != 2:
        return lax.all_gather(weight, "dp", axis=0, tiled=True)
    other = lax.ppermute(weight, "dp", [(0, 1), (1, 0)])
    return ordered_pair(weight, other, "dp", 0)


def summed_rows(term):
    group = ("ctx", "dp")
    count = lax.axis_size(group)
    parts = lax.all_to_all(term, group, 0, 0, tiled=True)
    parts = parts.reshape(count, term.shape[0] // count, *term.shape[1:])
    return jnp.sum(parts.astype(jnp.float32), axis=0)


def section_sum(partial):
    count = lax.axis_size("section")
    if count != 2:
        return lax.psum(partial.astype(jnp.bfloat16), "section")
    mine = partial.astype(jnp.bfloat16)
    other = lax.ppermute(mine, "section", [(0, 1), (1, 0)])
    return (mine.astype(jnp.float32) + other.astype(jnp.float32)).astype(jnp.bfloat16)


def softmax_stats(scores, seen):
    row_top = jnp.max(jnp.where(seen, scores, -jnp.inf), axis=2, keepdims=True)
    raised = jnp.where(seen, jnp.exp(scores - row_top), 0.0)
    row_total = jnp.sum(raised, axis=2, keepdims=True)
    return raised / row_total, row_top, row_total


def per_device(normed, w_query, w_key, w_value, block_mask, cotangent):
    tokens = normed[0]
    upstream = cotangent[0]
    length = tokens.shape[0]
    features = upstream.shape[1]
    heads = features // HD
    blocks = length // BLOCK
    span_len = 2 * REACH + 1
    halo = REACH * BLOCK
    frame_blocks = blocks + 2 * REACH
    score_scale = HD ** (-0.5)

    left_tokens, right_tokens = neighbour_tokens(tokens, halo)
    query_full = full_rows(w_query)
    gathered = lax.all_gather(jnp.stack([w_key, w_value]), "dp", axis=1, tiled=True)
    key_full, value_full = gathered[0], gathered[1]

    frame_tokens = jnp.concatenate([left_tokens, tokens, right_tokens], axis=0)
    all_weights = jnp.concatenate([query_full, key_full, value_full], axis=1)
    frame_proj = jnp.dot(frame_tokens, all_weights, preferred_element_type=jnp.float32).astype(
        jnp.bfloat16
    )
    frame_proj, up_head, up_tail = lax.optimization_barrier(
        (frame_proj, upstream[:halo], upstream[length - halo :])
    )
    left_up = shifted(up_tail, "ctx", 1)
    right_up = shifted(up_head, "ctx", -1)
    query_h = head_major(frame_proj[:, :features], heads)
    key_h = head_major(frame_proj[:, features : 2 * features], heads)
    value_h = head_major(frame_proj[:, 2 * features :], heads)
    own_upstream = head_major(upstream, heads)
    near_upstream = head_major(jnp.concatenate([left_up, right_up], axis=0), heads)

    first_block = lax.axis_index("ctx") * blocks
    padded_mask = jnp.pad(block_mask, ((REACH, REACH), (0, 0)))
    frame_mask = lax.dynamic_slice(padded_mask, (first_block, 0), (frame_blocks, span_len))

    def rows(cells, at, count=1):
        return cells[:, at * BLOCK : (at + count) * BLOCK]

    def seen_keys(at, low, high):
        picked = frame_mask[at, low - at + REACH : high - at + REACH + 1] > 0
        return jnp.repeat(picked, BLOCK)[None, None, :]

    own_low, own_high = REACH, REACH + blocks - 1
    outs, query_grads, tops, totals, deltas = [], [], [], [], []
    own_score_grads, own_weights = [], []
    for i in range(blocks):
        at = REACH + i
        query_block = rows(query_h, at)
        upstream_block = rows(own_upstream, i)
        key_window = rows(key_h, i, span_len)
        value_window = rows(value_h, i, span_len)
        scores = (
            jnp.einsum("hqd,hkd->hqk", query_block, key_window, preferred_element_type=jnp.float32)
            * score_scale
        )
        probability, row_top, row_total = softmax_stats(scores, seen_keys(at, i, i + 2 * REACH))
        weights = probability.astype(jnp.bfloat16)
        outs.append(
            jnp.einsum("hqk,hkd->hqd", weights, value_window, preferred_element_type=jnp.float32)
        )
        prob_grad = jnp.einsum(
            "hqd,hkd->hqk", upstream_block, value_window, preferred_element_type=jnp.float32
        )
        row_delta = jnp.sum(probability * prob_grad, axis=2, keepdims=True)
        score_grad = (probability * (prob_grad - row_delta)).astype(jnp.bfloat16)
        query_grads.append(
            score_scale
            * jnp.einsum("hqk,hkd->hqd", score_grad, key_window, preferred_element_type=jnp.float32)
        )
        tops.append(row_top)
        totals.append(row_total)
        deltas.append(row_delta)
        cut = slice((own_low - i) * BLOCK, (own_high - i + 1) * BLOCK)
        own_score_grads.append(score_grad[:, :, cut])
        own_weights.append(weights[:, :, cut])

    attended = token_major(jnp.concatenate(outs, axis=1).astype(jnp.bfloat16))[None]
    query_grad = token_major(jnp.concatenate(query_grads, axis=1).astype(jnp.bfloat16))

    term_query = jnp.einsum(
        "tr,tf->rf", tokens, query_grad, preferred_element_type=jnp.float32
    ).astype(jnp.bfloat16)
    reduced_query = summed_rows(term_query)

    stats = jnp.stack(
        [jnp.concatenate(tops, axis=1), jnp.concatenate(totals, axis=1), jnp.concatenate(deltas, axis=1)]
    )
    stats_left = shifted(stats[:, :, length - halo :], "ctx", 1)
    stats_right = shifted(stats[:, :, :halo], "ctx", -1)

    near = list(range(REACH)) + list(range(REACH + blocks, frame_blocks))
    allowed = []
    for at in near:
        row = []
        for block in range(own_low, own_high + 1):
            slot = block - at + REACH
            row.append(frame_mask[at, slot] > 0 if 0 <= slot < span_len else jnp.zeros((), bool))
        allowed.append(jnp.stack(row))
    allowed = jnp.repeat(jnp.repeat(jnp.stack(allowed), BLOCK, axis=0), BLOCK, axis=1)[None]
    near_stats = jnp.concatenate([stats_left, stats_right], axis=2)
    top, total, delta = near_stats[0], near_stats[1], near_stats[2]
    near_query = jnp.concatenate([rows(query_h, 0, REACH), rows(query_h, REACH + blocks, REACH)], axis=1)
    key_part = rows(key_h, own_low, blocks)
    value_part = rows(value_h, own_low, blocks)
    scores = (
        jnp.einsum("hqd,hkd->hqk", near_query, key_part, preferred_element_type=jnp.float32)
        * score_scale
    )
    probability = jnp.where(allowed, jnp.exp(scores - top) / total, 0.0)
    weights = probability.astype(jnp.bfloat16)
    prob_grad = jnp.einsum(
        "hqd,hkd->hqk", near_upstream, value_part, preferred_element_type=jnp.float32
    )
    score_grad = (probability * (prob_grad - delta)).astype(jnp.bfloat16)
    all_score_grads = jnp.concatenate(own_score_grads + [score_grad], axis=1)
    all_weights = jnp.concatenate(own_weights + [weights], axis=1)
    all_queries = jnp.concatenate([rows(query_h, REACH, blocks), near_query], axis=1)
    all_upstream = jnp.concatenate([own_upstream, near_upstream], axis=1)
    key_own = score_scale * jnp.einsum(
        "hqk,hqd->hkd", all_score_grads, all_queries, preferred_element_type=jnp.float32
    )
    value_own = jnp.einsum(
        "hqk,hqd->hkd", all_weights, all_upstream, preferred_element_type=jnp.float32
    )

    key_grad = token_major(key_own).astype(jnp.bfloat16)
    value_grad = token_major(value_own).astype(jnp.bfloat16)

    contract = (((1,), (1,)), ((), ()))
    partial_input = (
        lax.dot_general(query_grad, query_full, contract, preferred_element_type=jnp.float32)
        + lax.dot_general(key_grad, key_full, contract, preferred_element_type=jnp.float32)
        + lax.dot_general(value_grad, value_full, contract, preferred_element_type=jnp.float32)
    )
    grad_input = section_sum(partial_input)[None]

    term_kv = jnp.einsum(
        "tr,tf->rf",
        tokens,
        jnp.concatenate([key_grad, value_grad], axis=1),
        preferred_element_type=jnp.float32,
    ).astype(jnp.bfloat16)
    reduced_kv = summed_rows(term_kv).reshape(-1, 2, features)
    summed = jnp.concatenate([reduced_query[:, None], reduced_kv], axis=1)
    grad_weights = summed / lax.axis_size("dp")
    return (attended, grad_input, grad_weights)


def solution(mesh):
    in_specs = (
        P("dp", "ctx", None),
        P("dp", "section"),
        P("dp", "section"),
        P("dp", "section"),
        P(),
        P("dp", "ctx", "section"),
    )
    out_specs = (P("dp", "ctx", "section"), P("dp", "ctx", None), P(("ctx", "dp"), None, "section"))
    return jax.shard_map(
        per_device, mesh=mesh, in_specs=in_specs, out_specs=out_specs, check_vma=False
    )
```

```python
import jax
import jax.numpy as jnp
from jax import lax
from jax.sharding import PartitionSpec as P

HD = 64
BLOCK = 128
REACH = 3


def shifted(value, axis, steps):
    count = lax.axis_size(axis)
    leading, last = (max(0, -steps), min(count, count - steps))
    return lax.ppermute(value, axis, [(source, source + steps) for source in range(leading, last)])


def head_major(rows, heads):
    return rows.reshape(rows.shape[0], heads, HD).transpose(1, 0, 2)


def token_major(cells):
    return cells.transpose(1, 0, 2).reshape(cells.shape[1], cells.shape[0] * cells.shape[2])


def ordered_pair(mine, other, axis, dim):
    first = lax.axis_index(axis) == 0
    return jnp.where(
        first,
        jnp.concatenate([mine, other], axis=dim),
        jnp.concatenate([other, mine], axis=dim),
    )


def neighbour_tokens(tokens, halo):
    count = lax.axis_size("section")
    if count != 2:
        return (shifted(tokens[-halo:], "ctx", 1), shifted(tokens[:halo], "ctx", -1))
    half = tokens.shape[1] // 2
    start = lax.axis_index("section") * half
    share = lax.dynamic_slice_in_dim(tokens, start, half, 1)
    fetched = jnp.stack([shifted(share[-halo:], "ctx", 1), shifted(share[:halo], "ctx", -1)])
    partner = lax.ppermute(fetched, "section", [(0, 1), (1, 0)])
    both = ordered_pair(fetched, partner, "section", 2)
    return (both[0], both[1])


def full_rows(weight):
    if lax.axis_size("dp") != 2:
        return lax.all_gather(weight, "dp", axis=0, tiled=True)
    other = lax.ppermute(weight, "dp", [(0, 1), (1, 0)])
    return ordered_pair(weight, other, "dp", 0)


def summed_rows(term):
    group = ("ctx", "dp")
    count = lax.axis_size(group)
    parts = lax.all_to_all(term, group, 0, 0, tiled=True)
    parts = parts.reshape(count, term.shape[0] // count, *term.shape[1:])
    return jnp.sum(parts.astype(jnp.float32), axis=0)


def section_sum(partial):
    count = lax.axis_size("section")
    if count != 2:
        return lax.psum(partial.astype(jnp.bfloat16), "section")
    mine = partial.astype(jnp.bfloat16)
    other = lax.ppermute(mine, "section", [(0, 1), (1, 0)])
    return (mine.astype(jnp.float32) + other.astype(jnp.float32)).astype(jnp.bfloat16)


def softmax_stats(scores, seen):
    row_top = jnp.max(jnp.where(seen, scores, -jnp.inf), axis=2, keepdims=True)
    raised = jnp.where(seen, jnp.exp(scores - row_top), 0.0)
    row_total = jnp.sum(raised, axis=2, keepdims=True)
    return raised / row_total, row_top, row_total


def per_device(normed, w_query, w_key, w_value, block_mask, cotangent):
    tokens = normed[0]
    upstream = cotangent[0]
    length = tokens.shape[0]
    features = upstream.shape[1]
    heads = features // HD
    blocks = length // BLOCK
    span_len = 2 * REACH + 1
    halo = REACH * BLOCK
    frame_blocks = blocks + 2 * REACH
    score_scale = HD ** (-0.5)

    left_tokens, right_tokens = neighbour_tokens(tokens, halo)
    query_full = full_rows(w_query)
    gathered = lax.all_gather(jnp.stack([w_key, w_value]), "dp", axis=1, tiled=True)
    key_full, value_full = gathered[0], gathered[1]

    frame_tokens = jnp.concatenate([left_tokens, tokens, right_tokens], axis=0)
    all_weights = jnp.concatenate([query_full, key_full, value_full], axis=1)
    frame_proj = jnp.dot(frame_tokens, all_weights, preferred_element_type=jnp.float32).astype(
        jnp.bfloat16
    )
    frame_proj, up_head, up_tail = lax.optimization_barrier(
        (frame_proj, upstream[:halo], upstream[length - halo :])
    )
    left_up = shifted(up_tail, "ctx", 1)
    right_up = shifted(up_head, "ctx", -1)
    query_h = head_major(frame_proj[:, :features], heads)
    key_h = head_major(frame_proj[:, features : 2 * features], heads)
    value_h = head_major(frame_proj[:, 2 * features :], heads)
    own_upstream = head_major(upstream, heads)
    near_upstream = head_major(jnp.concatenate([left_up, right_up], axis=0), heads)

    first_block = lax.axis_index("ctx") * blocks
    padded_mask = jnp.pad(block_mask, ((REACH, REACH), (0, 0)))
    frame_mask = lax.dynamic_slice(padded_mask, (first_block, 0), (frame_blocks, span_len))

    def rows(cells, at, count=1):
        return cells[:, at * BLOCK : (at + count) * BLOCK]

    def seen_keys(at, low, high):
        picked = frame_mask[at, low - at + REACH : high - at + REACH + 1] > 0
        return jnp.repeat(picked, BLOCK)[None, None, :]

    own_low, own_high = REACH, REACH + blocks - 1
    near = list(range(REACH)) + list(range(REACH + blocks, frame_blocks))
    allowed = []
    for at in near:
        row = []
        for block in range(own_low, own_high + 1):
            slot = block - at + REACH
            row.append(frame_mask[at, slot] > 0 if 0 <= slot < span_len else jnp.zeros((), bool))
        allowed.append(jnp.stack(row))
    allowed = jnp.repeat(jnp.repeat(jnp.stack(allowed), BLOCK, axis=0), BLOCK, axis=1)[None]

    def group_pass(query_g, key_g, value_g, own_up_g, near_up_g):
        outs, query_grads, tops, totals, deltas = [], [], [], [], []
        own_score_grads, own_weights = [], []
        for i in range(blocks):
            at = REACH + i
            query_block = rows(query_g, at)
            upstream_block = rows(own_up_g, i)
            key_window = rows(key_g, i, span_len)
            value_window = rows(value_g, i, span_len)
            scores = (
                jnp.einsum(
                    "hqd,hkd->hqk", query_block, key_window, preferred_element_type=jnp.float32
                )
                * score_scale
            )
            probability, row_top, row_total = softmax_stats(scores, seen_keys(at, i, i + 2 * REACH))
            weights = probability.astype(jnp.bfloat16)
            outs.append(
                jnp.einsum("hqk,hkd->hqd", weights, value_window, preferred_element_type=jnp.float32)
            )
            prob_grad = jnp.einsum(
                "hqd,hkd->hqk", upstream_block, value_window, preferred_element_type=jnp.float32
            )
            row_delta = jnp.sum(probability * prob_grad, axis=2, keepdims=True)
            score_grad = (probability * (prob_grad - row_delta)).astype(jnp.bfloat16)
            query_grads.append(
                score_scale
                * jnp.einsum(
                    "hqk,hkd->hqd", score_grad, key_window, preferred_element_type=jnp.float32
                )
            )
            tops.append(row_top)
            totals.append(row_total)
            deltas.append(row_delta)
            cut = slice((own_low - i) * BLOCK, (own_high - i + 1) * BLOCK)
            own_score_grads.append(score_grad[:, :, cut])
            own_weights.append(weights[:, :, cut])

        out_g = jnp.concatenate(outs, axis=1).astype(jnp.bfloat16)
        query_grad_g = jnp.concatenate(query_grads, axis=1).astype(jnp.bfloat16)
        term_query_g = summed_rows(
            jnp.einsum(
                "tr,tf->rf", tokens, token_major(query_grad_g), preferred_element_type=jnp.float32
            ).astype(jnp.bfloat16)
        )

        stats = jnp.stack(
            [
                jnp.concatenate(tops, axis=1),
                jnp.concatenate(totals, axis=1),
                jnp.concatenate(deltas, axis=1),
            ]
        )
        stats_left = shifted(stats[:, :, length - halo :], "ctx", 1)
        stats_right = shifted(stats[:, :, :halo], "ctx", -1)
        near_stats = jnp.concatenate([stats_left, stats_right], axis=2)
        top, total, delta = near_stats[0], near_stats[1], near_stats[2]
        near_query = jnp.concatenate(
            [rows(query_g, 0, REACH), rows(query_g, REACH + blocks, REACH)], axis=1
        )
        key_part = rows(key_g, own_low, blocks)
        value_part = rows(value_g, own_low, blocks)
        scores = (
            jnp.einsum("hqd,hkd->hqk", near_query, key_part, preferred_element_type=jnp.float32)
            * score_scale
        )
        probability = jnp.where(allowed, jnp.exp(scores - top) / total, 0.0)
        weights = probability.astype(jnp.bfloat16)
        prob_grad = jnp.einsum(
            "hqd,hkd->hqk", near_up_g, value_part, preferred_element_type=jnp.float32
        )
        score_grad = (probability * (prob_grad - delta)).astype(jnp.bfloat16)
        all_score_grads = jnp.concatenate(own_score_grads + [score_grad], axis=1)
        all_weights = jnp.concatenate(own_weights + [weights], axis=1)
        all_queries = jnp.concatenate([rows(query_g, REACH, blocks), near_query], axis=1)
        all_upstream = jnp.concatenate([own_up_g, near_up_g], axis=1)
        key_own = score_scale * jnp.einsum(
            "hqk,hqd->hkd", all_score_grads, all_queries, preferred_element_type=jnp.float32
        )
        value_own = jnp.einsum(
            "hqk,hqd->hkd", all_weights, all_upstream, preferred_element_type=jnp.float32
        )
        key_grad_g = token_major(key_own).astype(jnp.bfloat16)
        value_grad_g = token_major(value_own).astype(jnp.bfloat16)
        term_kv_g = summed_rows(
            jnp.einsum(
                "tr,tf->rf",
                tokens,
                jnp.concatenate([key_grad_g, value_grad_g], axis=1),
                preferred_element_type=jnp.float32,
            ).astype(jnp.bfloat16)
        )
        return out_g, query_grad_g, key_grad_g, value_grad_g, term_query_g, term_kv_g

    groups = 2 if heads % 2 == 0 else 1
    size = heads // groups
    results = []
    for g in range(groups):
        pick = slice(g * size, (g + 1) * size)
        results.append(
            group_pass(query_h[pick], key_h[pick], value_h[pick], own_upstream[pick], near_upstream[pick])
        )
    out_all = jnp.concatenate([r[0] for r in results], axis=0)
    attended = token_major(out_all)[None]
    query_grad = token_major(jnp.concatenate([r[1] for r in results], axis=0))
    key_grad = jnp.concatenate([r[2] for r in results], axis=1)
    value_grad = jnp.concatenate([r[3] for r in results], axis=1)
    width = size * HD
    reduced_query = jnp.concatenate([r[4] for r in results], axis=1)
    reduced_key = jnp.concatenate([r[5][:, :width] for r in results], axis=1)
    reduced_value = jnp.concatenate([r[5][:, width:] for r in results], axis=1)

    contract = (((1,), (1,)), ((), ()))
    partial_input = (
        lax.dot_general(query_grad, query_full, contract, preferred_element_type=jnp.float32)
        + lax.dot_general(key_grad, key_full, contract, preferred_element_type=jnp.float32)
        + lax.dot_general(value_grad, value_full, contract, preferred_element_type=jnp.float32)
    )
    grad_input = section_sum(partial_input)[None]

    summed = jnp.stack([reduced_query, reduced_key, reduced_value], axis=1)
    grad_weights = summed / lax.axis_size("dp")
    return (attended, grad_input, grad_weights)


def solution(mesh):
    in_specs = (
        P("dp", "ctx", None),
        P("dp", "section"),
        P("dp", "section"),
        P("dp", "section"),
        P(),
        P("dp", "ctx", "section"),
    )
    out_specs = (P("dp", "ctx", "section"), P("dp", "ctx", None), P(("ctx", "dp"), None, "section"))
    return jax.shard_map(
        per_device, mesh=mesh, in_specs=in_specs, out_specs=out_specs, check_vma=False
    )
```

```python
import jax
import jax.numpy as jnp
from jax import lax
from jax.sharding import PartitionSpec as P

HD = 64
BLOCK = 128
REACH = 3


def shifted(value, axis, steps):
    count = lax.axis_size(axis)
    leading, last = (max(0, -steps), min(count, count - steps))
    return lax.ppermute(value, axis, [(source, source + steps) for source in range(leading, last)])


def head_major(rows, heads):
    return rows.reshape(rows.shape[0], heads, HD).transpose(1, 0, 2)


def token_major(cells):
    return cells.transpose(1, 0, 2).reshape(cells.shape[1], cells.shape[0] * cells.shape[2])


def ordered_pair(mine, other, axis, dim):
    first = lax.axis_index(axis) == 0
    return jnp.where(
        first,
        jnp.concatenate([mine, other], axis=dim),
        jnp.concatenate([other, mine], axis=dim),
    )


def neighbour_tokens(tokens, halo):
    count = lax.axis_size("section")
    if count != 2:
        return (shifted(tokens[-halo:], "ctx", 1), shifted(tokens[:halo], "ctx", -1))
    half = tokens.shape[1] // 2
    start = lax.axis_index("section") * half
    share = lax.dynamic_slice_in_dim(tokens, start, half, 1)
    fetched = jnp.stack([shifted(share[-halo:], "ctx", 1), shifted(share[:halo], "ctx", -1)])
    partner = lax.ppermute(fetched, "section", [(0, 1), (1, 0)])
    both = ordered_pair(fetched, partner, "section", 2)
    return (both[0], both[1])


def full_rows(weight):
    if lax.axis_size("dp") != 2:
        return lax.all_gather(weight, "dp", axis=0, tiled=True)
    other = lax.ppermute(weight, "dp", [(0, 1), (1, 0)])
    return ordered_pair(weight, other, "dp", 0)


def summed_rows(term):
    group = ("ctx", "dp")
    count = lax.axis_size(group)
    parts = lax.all_to_all(term, group, 0, 0, tiled=True)
    parts = parts.reshape(count, term.shape[0] // count, *term.shape[1:])
    return jnp.sum(parts.astype(jnp.float32), axis=0)


def section_sum(partial):
    count = lax.axis_size("section")
    if count != 2:
        return lax.psum(partial.astype(jnp.bfloat16), "section")
    mine = partial.astype(jnp.bfloat16)
    other = lax.ppermute(mine, "section", [(0, 1), (1, 0)])
    return (mine.astype(jnp.float32) + other.astype(jnp.float32)).astype(jnp.bfloat16)


def softmax_stats(scores, seen):
    row_top = jnp.max(jnp.where(seen, scores, -jnp.inf), axis=2, keepdims=True)
    raised = jnp.where(seen, jnp.exp(scores - row_top), 0.0)
    row_total = jnp.sum(raised, axis=2, keepdims=True)
    return raised / row_total, row_top, row_total


def per_device(normed, w_query, w_key, w_value, block_mask, cotangent):
    tokens = normed[0]
    upstream = cotangent[0]
    length = tokens.shape[0]
    features = upstream.shape[1]
    heads = features // HD
    blocks = length // BLOCK
    span_len = 2 * REACH + 1
    halo = REACH * BLOCK
    frame_blocks = blocks + 2 * REACH
    score_scale = HD ** (-0.5)

    left_tokens, right_tokens = neighbour_tokens(tokens, halo)
    left_up = shifted(upstream[length - halo :], "ctx", 1)
    right_up = shifted(upstream[:halo], "ctx", -1)
    gathered = lax.all_gather(jnp.stack([w_query, w_key, w_value]), "dp", axis=1, tiled=True)
    query_full, key_full, value_full = gathered[0], gathered[1], gathered[2]

    frame_tokens = jnp.concatenate([left_tokens, tokens, right_tokens], axis=0)
    all_weights = jnp.concatenate([query_full, key_full, value_full], axis=1)
    frame_proj = jnp.dot(frame_tokens, all_weights, preferred_element_type=jnp.float32).astype(
        jnp.bfloat16
    )
    query_h = head_major(frame_proj[:, :features], heads)
    key_h = head_major(frame_proj[:, features : 2 * features], heads)
    value_h = head_major(frame_proj[:, 2 * features :], heads)
    own_upstream = head_major(upstream, heads)
    near_upstream = head_major(jnp.concatenate([left_up, right_up], axis=0), heads)

    first_block = lax.axis_index("ctx") * blocks
    padded_mask = jnp.pad(block_mask, ((REACH, REACH), (0, 0)))
    frame_mask = lax.dynamic_slice(padded_mask, (first_block, 0), (frame_blocks, span_len))

    def rows(cells, at, count=1):
        return cells[:, at * BLOCK : (at + count) * BLOCK]

    def seen_keys(at, low, high):
        picked = frame_mask[at, low - at + REACH : high - at + REACH + 1] > 0
        return jnp.repeat(picked, BLOCK)[None, None, :]

    own_low, own_high = REACH, REACH + blocks - 1
    outs, query_grads, tops, totals, deltas = [], [], [], [], []
    own_score_grads, own_weights = [], []
    for i in range(blocks):
        at = REACH + i
        query_block = rows(query_h, at)
        upstream_block = rows(own_upstream, i)
        key_window = rows(key_h, i, span_len)
        value_window = rows(value_h, i, span_len)
        scores = (
            jnp.einsum("hqd,hkd->hqk", query_block, key_window, preferred_element_type=jnp.float32)
            * score_scale
        )
        probability, row_top, row_total = softmax_stats(scores, seen_keys(at, i, i + 2 * REACH))
        weights = probability.astype(jnp.bfloat16)
        outs.append(
            jnp.einsum("hqk,hkd->hqd", weights, value_window, preferred_element_type=jnp.float32)
        )
        prob_grad = jnp.einsum(
            "hqd,hkd->hqk", upstream_block, value_window, preferred_element_type=jnp.float32
        )
        row_delta = jnp.sum(probability * prob_grad, axis=2, keepdims=True)
        score_grad = (probability * (prob_grad - row_delta)).astype(jnp.bfloat16)
        query_grads.append(
            score_scale
            * jnp.einsum("hqk,hkd->hqd", score_grad, key_window, preferred_element_type=jnp.float32)
        )
        tops.append(row_top)
        totals.append(row_total)
        deltas.append(row_delta)
        cut = slice((own_low - i) * BLOCK, (own_high - i + 1) * BLOCK)
        own_score_grads.append(score_grad[:, :, cut])
        own_weights.append(weights[:, :, cut])

    attended = token_major(jnp.concatenate(outs, axis=1).astype(jnp.bfloat16))[None]
    query_grad = token_major(jnp.concatenate(query_grads, axis=1).astype(jnp.bfloat16))

    term_query = jnp.einsum(
        "tr,tf->rf", tokens, query_grad, preferred_element_type=jnp.float32
    ).astype(jnp.bfloat16)
    reduced_query = summed_rows(term_query)

    stats = jnp.stack(
        [jnp.concatenate(tops, axis=1), jnp.concatenate(totals, axis=1), jnp.concatenate(deltas, axis=1)]
    )
    stats_left = shifted(stats[:, :, length - halo :], "ctx", 1)
    stats_right = shifted(stats[:, :, :halo], "ctx", -1)

    near = list(range(REACH)) + list(range(REACH + blocks, frame_blocks))
    allowed = []
    for at in near:
        row = []
        for block in range(own_low, own_high + 1):
            slot = block - at + REACH
            row.append(frame_mask[at, slot] > 0 if 0 <= slot < span_len else jnp.zeros((), bool))
        allowed.append(jnp.stack(row))
    allowed = jnp.repeat(jnp.repeat(jnp.stack(allowed), BLOCK, axis=0), BLOCK, axis=1)[None]
    near_stats = jnp.concatenate([stats_left, stats_right], axis=2)
    top, total, delta = near_stats[0], near_stats[1], near_stats[2]
    near_query = jnp.concatenate([rows(query_h, 0, REACH), rows(query_h, REACH + blocks, REACH)], axis=1)
    key_part = rows(key_h, own_low, blocks)
    value_part = rows(value_h, own_low, blocks)
    scores = (
        jnp.einsum("hqd,hkd->hqk", near_query, key_part, preferred_element_type=jnp.float32)
        * score_scale
    )
    probability = jnp.where(allowed, jnp.exp(scores - top) / total, 0.0)
    weights = probability.astype(jnp.bfloat16)
    prob_grad = jnp.einsum(
        "hqd,hkd->hqk", near_upstream, value_part, preferred_element_type=jnp.float32
    )
    score_grad = (probability * (prob_grad - delta)).astype(jnp.bfloat16)
    all_score_grads = jnp.concatenate(own_score_grads + [score_grad], axis=1)
    all_weights = jnp.concatenate(own_weights + [weights], axis=1)
    all_queries = jnp.concatenate([rows(query_h, REACH, blocks), near_query], axis=1)
    all_upstream = jnp.concatenate([own_upstream, near_upstream], axis=1)
    key_own = score_scale * jnp.einsum(
        "hqk,hqd->hkd", all_score_grads, all_queries, preferred_element_type=jnp.float32
    )
    value_own = jnp.einsum(
        "hqk,hqd->hkd", all_weights, all_upstream, preferred_element_type=jnp.float32
    )

    key_grad = token_major(key_own).astype(jnp.bfloat16)
    value_grad = token_major(value_own).astype(jnp.bfloat16)

    contract = (((1,), (1,)), ((), ()))
    partial_input = (
        lax.dot_general(query_grad, query_full, contract, preferred_element_type=jnp.float32)
        + lax.dot_general(key_grad, key_full, contract, preferred_element_type=jnp.float32)
        + lax.dot_general(value_grad, value_full, contract, preferred_element_type=jnp.float32)
    )
    grad_input = section_sum(partial_input)[None]

    term_kv = jnp.einsum(
        "tr,tf->rf",
        tokens,
        jnp.concatenate([key_grad, value_grad], axis=1),
        preferred_element_type=jnp.float32,
    ).astype(jnp.bfloat16)
    reduced_kv = summed_rows(term_kv).reshape(-1, 2, features)
    summed = jnp.concatenate([reduced_query[:, None], reduced_kv], axis=1)
    grad_weights = summed / lax.axis_size("dp")
    return (attended, grad_input, grad_weights)


def solution(mesh):
    in_specs = (
        P("dp", "ctx", None),
        P("dp", "section"),
        P("dp", "section"),
        P("dp", "section"),
        P(),
        P("dp", "ctx", "section"),
    )
    out_specs = (P("dp", "ctx", "section"), P("dp", "ctx", None), P(("ctx", "dp"), None, "section"))
    return jax.shard_map(
        per_device, mesh=mesh, in_specs=in_specs, out_specs=out_specs, check_vma=False
    )
```

```python
import jax
import jax.numpy as jnp
from jax import lax
from jax.sharding import PartitionSpec as P

HD = 64
BLOCK = 128
REACH = 3


def shifted(value, axis, steps):
    count = lax.axis_size(axis)
    leading, last = (max(0, -steps), min(count, count - steps))
    return lax.ppermute(value, axis, [(source, source + steps) for source in range(leading, last)])


def head_major(rows, heads):
    return rows.reshape(rows.shape[0], heads, HD).transpose(1, 0, 2)


def token_major(cells):
    return cells.transpose(1, 0, 2).reshape(cells.shape[1], cells.shape[0] * cells.shape[2])


def ordered_pair(mine, other, axis, dim):
    first = lax.axis_index(axis) == 0
    return jnp.where(
        first,
        jnp.concatenate([mine, other], axis=dim),
        jnp.concatenate([other, mine], axis=dim),
    )


def neighbour_tokens(tokens, halo):
    count = lax.axis_size("section")
    if count != 2:
        return (shifted(tokens[-halo:], "ctx", 1), shifted(tokens[:halo], "ctx", -1))
    half = tokens.shape[1] // 2
    start = lax.axis_index("section") * half
    share = lax.dynamic_slice_in_dim(tokens, start, half, 1)
    fetched = jnp.stack([shifted(share[-halo:], "ctx", 1), shifted(share[:halo], "ctx", -1)])
    partner = lax.ppermute(fetched, "section", [(0, 1), (1, 0)])
    both = ordered_pair(fetched, partner, "section", 2)
    return (both[0], both[1])


def full_rows(weight):
    if lax.axis_size("dp") != 2:
        return lax.all_gather(weight, "dp", axis=0, tiled=True)
    other = lax.ppermute(weight, "dp", [(0, 1), (1, 0)])
    return ordered_pair(weight, other, "dp", 0)


def summed_rows(term):
    group = ("ctx", "dp")
    count = lax.axis_size(group)
    parts = lax.all_to_all(term, group, 0, 0, tiled=True)
    parts = parts.reshape(count, term.shape[0] // count, *term.shape[1:])
    return jnp.sum(parts.astype(jnp.float32), axis=0)


def section_sum(partial):
    count = lax.axis_size("section")
    if count != 2:
        return lax.psum(partial.astype(jnp.bfloat16), "section")
    mine = partial.astype(jnp.bfloat16)
    other = lax.ppermute(mine, "section", [(0, 1), (1, 0)])
    return (mine.astype(jnp.float32) + other.astype(jnp.float32)).astype(jnp.bfloat16)


def softmax_stats(scores, seen):
    row_top = jnp.max(jnp.where(seen, scores, -jnp.inf), axis=2, keepdims=True)
    raised = jnp.where(seen, jnp.exp(scores - row_top), 0.0)
    row_total = jnp.sum(raised, axis=2, keepdims=True)
    return raised / row_total, row_top, row_total


def per_device(normed, w_query, w_key, w_value, block_mask, cotangent):
    tokens = normed[0]
    upstream = cotangent[0]
    length = tokens.shape[0]
    features = upstream.shape[1]
    heads = features // HD
    blocks = length // BLOCK
    span_len = 2 * REACH + 1
    halo = REACH * BLOCK
    frame_blocks = blocks + 2 * REACH
    score_scale = HD ** (-0.5)

    left_tokens, right_tokens = neighbour_tokens(tokens, halo)
    left_up = shifted(upstream[length - halo :], "ctx", 1)
    right_up = shifted(upstream[:halo], "ctx", -1)
    gathered = lax.all_gather(jnp.stack([w_query, w_key, w_value]), "dp", axis=1, tiled=True)
    query_full, key_full, value_full = gathered[0], gathered[1], gathered[2]

    frame_tokens = jnp.concatenate([left_tokens, tokens, right_tokens], axis=0)
    all_weights = jnp.concatenate([query_full, key_full, value_full], axis=1)
    frame_proj = jnp.dot(frame_tokens, all_weights, preferred_element_type=jnp.float32).astype(
        jnp.bfloat16
    )
    query_h = head_major(frame_proj[:, :features], heads)
    key_h = head_major(frame_proj[:, features : 2 * features], heads)
    value_h = head_major(frame_proj[:, 2 * features :], heads)
    own_upstream = head_major(upstream, heads)
    near_upstream = head_major(jnp.concatenate([left_up, right_up], axis=0), heads)

    first_block = lax.axis_index("ctx") * blocks
    padded_mask = jnp.pad(block_mask, ((REACH, REACH), (0, 0)))
    frame_mask = lax.dynamic_slice(padded_mask, (first_block, 0), (frame_blocks, span_len))

    def rows(cells, at, count=1):
        return cells[:, at * BLOCK : (at + count) * BLOCK]

    def seen_keys(at, low, high):
        picked = frame_mask[at, low - at + REACH : high - at + REACH + 1] > 0
        return jnp.repeat(picked, BLOCK)[None, None, :]

    own_low, own_high = REACH, REACH + blocks - 1
    own_mask = frame_mask[REACH : REACH + blocks]

    def own_block(i):
        query_block = lax.dynamic_slice_in_dim(query_h, (REACH + i) * BLOCK, BLOCK, 1)
        upstream_block = lax.dynamic_slice_in_dim(own_upstream, i * BLOCK, BLOCK, 1)
        key_window = lax.dynamic_slice_in_dim(key_h, i * BLOCK, span_len * BLOCK, 1)
        value_window = lax.dynamic_slice_in_dim(value_h, i * BLOCK, span_len * BLOCK, 1)
        seen = jnp.repeat(lax.dynamic_index_in_dim(own_mask, i, 0, False) > 0, BLOCK)[None, None, :]
        scores = (
            jnp.einsum("hqd,hkd->hqk", query_block, key_window, preferred_element_type=jnp.float32)
            * score_scale
        )
        probability, row_top, row_total = softmax_stats(scores, seen)
        weights = probability.astype(jnp.bfloat16)
        out = jnp.einsum("hqk,hkd->hqd", weights, value_window, preferred_element_type=jnp.float32)
        prob_grad = jnp.einsum(
            "hqd,hkd->hqk", upstream_block, value_window, preferred_element_type=jnp.float32
        )
        row_delta = jnp.sum(probability * prob_grad, axis=2, keepdims=True)
        score_grad = (probability * (prob_grad - row_delta)).astype(jnp.bfloat16)
        query_grad = score_scale * jnp.einsum(
            "hqk,hkd->hqd", score_grad, key_window, preferred_element_type=jnp.float32
        )
        first = (own_low - i) * BLOCK
        own_grad = lax.dynamic_slice_in_dim(score_grad, first, blocks * BLOCK, 2)
        own_weight = lax.dynamic_slice_in_dim(weights, first, blocks * BLOCK, 2)
        return (
            out.astype(jnp.bfloat16),
            query_grad.astype(jnp.bfloat16),
            jnp.stack([row_top, row_total, row_delta]),
            own_grad,
            own_weight,
        )

    outs, query_grads, block_stats, own_grads, own_weights_all = lax.map(
        own_block, jnp.arange(blocks, dtype=jnp.int32)
    )

    attended = token_major(jnp.concatenate([outs[i] for i in range(blocks)], axis=1))[None]
    query_grad = token_major(jnp.concatenate([query_grads[i] for i in range(blocks)], axis=1))
    own_score_grads = [own_grads[i] for i in range(blocks)]
    own_weights = [own_weights_all[i] for i in range(blocks)]

    term_query = jnp.einsum(
        "tr,tf->rf", tokens, query_grad, preferred_element_type=jnp.float32
    ).astype(jnp.bfloat16)
    reduced_query = summed_rows(term_query)

    stats = jnp.concatenate([block_stats[i] for i in range(blocks)], axis=2)
    stats_left = shifted(stats[:, :, length - halo :], "ctx", 1)
    stats_right = shifted(stats[:, :, :halo], "ctx", -1)

    near = list(range(REACH)) + list(range(REACH + blocks, frame_blocks))
    allowed = []
    for at in near:
        row = []
        for block in range(own_low, own_high + 1):
            slot = block - at + REACH
            row.append(frame_mask[at, slot] > 0 if 0 <= slot < span_len else jnp.zeros((), bool))
        allowed.append(jnp.stack(row))
    allowed = jnp.repeat(jnp.repeat(jnp.stack(allowed), BLOCK, axis=0), BLOCK, axis=1)[None]
    near_stats = jnp.concatenate([stats_left, stats_right], axis=2)
    top, total, delta = near_stats[0], near_stats[1], near_stats[2]
    near_query = jnp.concatenate([rows(query_h, 0, REACH), rows(query_h, REACH + blocks, REACH)], axis=1)
    key_part = rows(key_h, own_low, blocks)
    value_part = rows(value_h, own_low, blocks)
    scores = (
        jnp.einsum("hqd,hkd->hqk", near_query, key_part, preferred_element_type=jnp.float32)
        * score_scale
    )
    probability = jnp.where(allowed, jnp.exp(scores - top) / total, 0.0)
    weights = probability.astype(jnp.bfloat16)
    prob_grad = jnp.einsum(
        "hqd,hkd->hqk", near_upstream, value_part, preferred_element_type=jnp.float32
    )
    score_grad = (probability * (prob_grad - delta)).astype(jnp.bfloat16)
    all_score_grads = jnp.concatenate(own_score_grads + [score_grad], axis=1)
    all_weights = jnp.concatenate(own_weights + [weights], axis=1)
    all_queries = jnp.concatenate([rows(query_h, REACH, blocks), near_query], axis=1)
    all_upstream = jnp.concatenate([own_upstream, near_upstream], axis=1)
    key_own = score_scale * jnp.einsum(
        "hqk,hqd->hkd", all_score_grads, all_queries, preferred_element_type=jnp.float32
    )
    value_own = jnp.einsum(
        "hqk,hqd->hkd", all_weights, all_upstream, preferred_element_type=jnp.float32
    )

    key_grad = token_major(key_own).astype(jnp.bfloat16)
    value_grad = token_major(value_own).astype(jnp.bfloat16)

    contract = (((1,), (1,)), ((), ()))
    partial_input = (
        lax.dot_general(query_grad, query_full, contract, preferred_element_type=jnp.float32)
        + lax.dot_general(key_grad, key_full, contract, preferred_element_type=jnp.float32)
        + lax.dot_general(value_grad, value_full, contract, preferred_element_type=jnp.float32)
    )
    grad_input = section_sum(partial_input)[None]

    term_kv = jnp.einsum(
        "tr,tf->rf",
        tokens,
        jnp.concatenate([key_grad, value_grad], axis=1),
        preferred_element_type=jnp.float32,
    ).astype(jnp.bfloat16)
    reduced_kv = summed_rows(term_kv).reshape(-1, 2, features)
    summed = jnp.concatenate([reduced_query[:, None], reduced_kv], axis=1)
    grad_weights = summed / lax.axis_size("dp")
    return (attended, grad_input, grad_weights)


def solution(mesh):
    in_specs = (
        P("dp", "ctx", None),
        P("dp", "section"),
        P("dp", "section"),
        P("dp", "section"),
        P(),
        P("dp", "ctx", "section"),
    )
    out_specs = (P("dp", "ctx", "section"), P("dp", "ctx", None), P(("ctx", "dp"), None, "section"))
    return jax.shard_map(
        per_device, mesh=mesh, in_specs=in_specs, out_specs=out_specs, check_vma=False
    )
```

```python
import jax
import jax.numpy as jnp
from jax import lax
from jax.sharding import PartitionSpec as P

HD = 64
BLOCK = 128
REACH = 3


def shifted(value, axis, steps):
    count = lax.axis_size(axis)
    leading, last = (max(0, -steps), min(count, count - steps))
    return lax.ppermute(value, axis, [(source, source + steps) for source in range(leading, last)])


def head_major(rows, heads):
    return rows.reshape(rows.shape[0], heads, HD).transpose(1, 0, 2)


def token_major(cells):
    return cells.transpose(1, 0, 2).reshape(cells.shape[1], cells.shape[0] * cells.shape[2])


def ordered_pair(mine, other, axis, dim):
    first = lax.axis_index(axis) == 0
    return jnp.where(
        first,
        jnp.concatenate([mine, other], axis=dim),
        jnp.concatenate([other, mine], axis=dim),
    )


def neighbour_tokens(tokens, halo):
    count = lax.axis_size("section")
    if count != 2:
        return (shifted(tokens[-halo:], "ctx", 1), shifted(tokens[:halo], "ctx", -1))
    half = tokens.shape[1] // 2
    start = lax.axis_index("section") * half
    share = lax.dynamic_slice_in_dim(tokens, start, half, 1)
    fetched = jnp.stack([shifted(share[-halo:], "ctx", 1), shifted(share[:halo], "ctx", -1)])
    partner = lax.ppermute(fetched, "section", [(0, 1), (1, 0)])
    both = ordered_pair(fetched, partner, "section", 2)
    return (both[0], both[1])


def full_rows(weight):
    if lax.axis_size("dp") != 2:
        return lax.all_gather(weight, "dp", axis=0, tiled=True)
    other = lax.ppermute(weight, "dp", [(0, 1), (1, 0)])
    return ordered_pair(weight, other, "dp", 0)


def summed_rows(term):
    group = ("ctx", "dp")
    count = lax.axis_size(group)
    parts = lax.all_to_all(term, group, 0, 0, tiled=True)
    parts = parts.reshape(count, term.shape[0] // count, *term.shape[1:])
    return jnp.sum(parts.astype(jnp.float32), axis=0)


def section_sum(partial):
    count = lax.axis_size("section")
    if count != 2:
        return lax.psum(partial.astype(jnp.bfloat16), "section")
    mine = partial.astype(jnp.bfloat16)
    other = lax.ppermute(mine, "section", [(0, 1), (1, 0)])
    return (mine.astype(jnp.float32) + other.astype(jnp.float32)).astype(jnp.bfloat16)


def softmax_stats(scores, seen):
    row_top = jnp.max(jnp.where(seen, scores, -jnp.inf), axis=2, keepdims=True)
    raised = jnp.where(seen, jnp.exp(scores - row_top), 0.0)
    row_total = jnp.sum(raised, axis=2, keepdims=True)
    return raised / row_total, row_top, row_total


def per_device(normed, w_query, w_key, w_value, block_mask, cotangent):
    tokens = normed[0]
    upstream = cotangent[0]
    length = tokens.shape[0]
    features = upstream.shape[1]
    heads = features // HD
    blocks = length // BLOCK
    span_len = 2 * REACH + 1
    halo = REACH * BLOCK
    frame_blocks = blocks + 2 * REACH
    score_scale = HD ** (-0.5)

    left_tokens, right_tokens = neighbour_tokens(tokens, halo)
    left_up = shifted(upstream[length - halo :], "ctx", 1)
    right_up = shifted(upstream[:halo], "ctx", -1)
    projection = lax.all_gather(
        jnp.concatenate([w_query, w_key, w_value], axis=1), "dp", axis=0, tiled=True
    )

    frame_tokens = jnp.concatenate([left_tokens, tokens, right_tokens], axis=0)
    frame_proj = jnp.dot(frame_tokens, projection, preferred_element_type=jnp.float32).astype(
        jnp.bfloat16
    )
    query_h = head_major(frame_proj[:, :features], heads)
    key_h = head_major(frame_proj[:, features : 2 * features], heads)
    value_h = head_major(frame_proj[:, 2 * features :], heads)
    own_upstream = head_major(upstream, heads)
    near_upstream = head_major(jnp.concatenate([left_up, right_up], axis=0), heads)

    first_block = lax.axis_index("ctx") * blocks
    padded_mask = jnp.pad(block_mask, ((REACH, REACH), (0, 0)))
    frame_mask = lax.dynamic_slice(padded_mask, (first_block, 0), (frame_blocks, span_len))

    def rows(cells, at, count=1):
        return cells[:, at * BLOCK : (at + count) * BLOCK]

    def seen_keys(at, low, high):
        picked = frame_mask[at, low - at + REACH : high - at + REACH + 1] > 0
        return jnp.repeat(picked, BLOCK)[None, None, :]

    own_low, own_high = REACH, REACH + blocks - 1
    outs, query_grads, tops, totals, deltas = [], [], [], [], []
    own_score_grads, own_weights = [], []
    for i in range(blocks):
        at = REACH + i
        query_block = rows(query_h, at)
        upstream_block = rows(own_upstream, i)
        key_window = rows(key_h, i, span_len)
        value_window = rows(value_h, i, span_len)
        scores = (
            jnp.einsum("hqd,hkd->hqk", query_block, key_window, preferred_element_type=jnp.float32)
            * score_scale
        )
        probability, row_top, row_total = softmax_stats(scores, seen_keys(at, i, i + 2 * REACH))
        weights = probability.astype(jnp.bfloat16)
        outs.append(
            jnp.einsum("hqk,hkd->hqd", weights, value_window, preferred_element_type=jnp.float32)
        )
        prob_grad = jnp.einsum(
            "hqd,hkd->hqk", upstream_block, value_window, preferred_element_type=jnp.float32
        )
        row_delta = jnp.sum(probability * prob_grad, axis=2, keepdims=True)
        score_grad = (probability * (prob_grad - row_delta)).astype(jnp.bfloat16)
        query_grads.append(
            score_scale
            * jnp.einsum("hqk,hkd->hqd", score_grad, key_window, preferred_element_type=jnp.float32)
        )
        tops.append(row_top)
        totals.append(row_total)
        deltas.append(row_delta)
        cut = slice((own_low - i) * BLOCK, (own_high - i + 1) * BLOCK)
        own_score_grads.append(score_grad[:, :, cut])
        own_weights.append(weights[:, :, cut])

    attended = token_major(jnp.concatenate(outs, axis=1).astype(jnp.bfloat16))[None]
    query_grad = token_major(jnp.concatenate(query_grads, axis=1).astype(jnp.bfloat16))

    term_query = jnp.einsum(
        "tr,tf->rf", tokens, query_grad, preferred_element_type=jnp.float32
    ).astype(jnp.bfloat16)
    reduced_query = summed_rows(term_query)

    stats = jnp.stack(
        [jnp.concatenate(tops, axis=1), jnp.concatenate(totals, axis=1), jnp.concatenate(deltas, axis=1)]
    )
    stats_left = shifted(stats[:, :, length - halo :], "ctx", 1)
    stats_right = shifted(stats[:, :, :halo], "ctx", -1)

    near = list(range(REACH)) + list(range(REACH + blocks, frame_blocks))
    allowed = []
    for at in near:
        row = []
        for block in range(own_low, own_high + 1):
            slot = block - at + REACH
            row.append(frame_mask[at, slot] > 0 if 0 <= slot < span_len else jnp.zeros((), bool))
        allowed.append(jnp.stack(row))
    allowed = jnp.repeat(jnp.repeat(jnp.stack(allowed), BLOCK, axis=0), BLOCK, axis=1)[None]
    near_stats = jnp.concatenate([stats_left, stats_right], axis=2)
    top, total, delta = near_stats[0], near_stats[1], near_stats[2]
    near_query = jnp.concatenate([rows(query_h, 0, REACH), rows(query_h, REACH + blocks, REACH)], axis=1)
    key_part = rows(key_h, own_low, blocks)
    value_part = rows(value_h, own_low, blocks)
    scores = (
        jnp.einsum("hqd,hkd->hqk", near_query, key_part, preferred_element_type=jnp.float32)
        * score_scale
    )
    probability = jnp.where(allowed, jnp.exp(scores - top) / total, 0.0)
    weights = probability.astype(jnp.bfloat16)
    prob_grad = jnp.einsum(
        "hqd,hkd->hqk", near_upstream, value_part, preferred_element_type=jnp.float32
    )
    score_grad = (probability * (prob_grad - delta)).astype(jnp.bfloat16)
    all_score_grads = jnp.concatenate(own_score_grads + [score_grad], axis=1)
    all_weights = jnp.concatenate(own_weights + [weights], axis=1)
    all_queries = jnp.concatenate([rows(query_h, REACH, blocks), near_query], axis=1)
    all_upstream = jnp.concatenate([own_upstream, near_upstream], axis=1)
    key_own = score_scale * jnp.einsum(
        "hqk,hqd->hkd", all_score_grads, all_queries, preferred_element_type=jnp.float32
    )
    value_own = jnp.einsum(
        "hqk,hqd->hkd", all_weights, all_upstream, preferred_element_type=jnp.float32
    )

    key_grad = token_major(key_own).astype(jnp.bfloat16)
    value_grad = token_major(value_own).astype(jnp.bfloat16)

    contract = (((1,), (1,)), ((), ()))
    partial_input = lax.dot_general(
        jnp.concatenate([query_grad, key_grad, value_grad], axis=1),
        projection,
        contract,
        preferred_element_type=jnp.float32,
    )
    grad_input = section_sum(partial_input)[None]

    term_kv = jnp.einsum(
        "tr,tf->rf",
        tokens,
        jnp.concatenate([key_grad, value_grad], axis=1),
        preferred_element_type=jnp.float32,
    ).astype(jnp.bfloat16)
    reduced_kv = summed_rows(term_kv).reshape(-1, 2, features)
    summed = jnp.concatenate([reduced_query[:, None], reduced_kv], axis=1)
    grad_weights = summed / lax.axis_size("dp")
    return (attended, grad_input, grad_weights)


def solution(mesh):
    in_specs = (
        P("dp", "ctx", None),
        P("dp", "section"),
        P("dp", "section"),
        P("dp", "section"),
        P(),
        P("dp", "ctx", "section"),
    )
    out_specs = (P("dp", "ctx", "section"), P("dp", "ctx", None), P(("ctx", "dp"), None, "section"))
    return jax.shard_map(
        per_device, mesh=mesh, in_specs=in_specs, out_specs=out_specs, check_vma=False
    )
```

```python
import jax
import jax.numpy as jnp
import numpy as np
from jax import lax
from jax.sharding import PartitionSpec as P

HD = 64
BLOCK = 128
REACH = 3


def shifted(value, axis, steps):
    count = lax.axis_size(axis)
    leading, last = (max(0, -steps), min(count, count - steps))
    return lax.ppermute(value, axis, [(source, source + steps) for source in range(leading, last)])


def head_major(rows, heads):
    return rows.reshape(rows.shape[0], heads, HD).transpose(1, 0, 2)


def token_major(cells):
    return cells.transpose(1, 0, 2).reshape(cells.shape[1], cells.shape[0] * cells.shape[2])


def ordered_pair(mine, other, axis, dim):
    first = lax.axis_index(axis) == 0
    return jnp.where(
        first,
        jnp.concatenate([mine, other], axis=dim),
        jnp.concatenate([other, mine], axis=dim),
    )


def neighbour_tokens(tokens, halo):
    count = lax.axis_size("section")
    if count != 2:
        return (shifted(tokens[-halo:], "ctx", 1), shifted(tokens[:halo], "ctx", -1))
    half = tokens.shape[1] // 2
    start = lax.axis_index("section") * half
    share = lax.dynamic_slice_in_dim(tokens, start, half, 1)
    fetched = jnp.stack([shifted(share[-halo:], "ctx", 1), shifted(share[:halo], "ctx", -1)])
    partner = lax.ppermute(fetched, "section", [(0, 1), (1, 0)])
    both = ordered_pair(fetched, partner, "section", 2)
    return (both[0], both[1])


def full_rows(weight):
    if lax.axis_size("dp") != 2:
        return lax.all_gather(weight, "dp", axis=0, tiled=True)
    other = lax.ppermute(weight, "dp", [(0, 1), (1, 0)])
    return ordered_pair(weight, other, "dp", 0)


def summed_rows(term):
    group = ("ctx", "dp")
    count = lax.axis_size(group)
    parts = lax.all_to_all(term, group, 0, 0, tiled=True)
    parts = parts.reshape(count, term.shape[0] // count, *term.shape[1:])
    return jnp.sum(parts.astype(jnp.float32), axis=0)


def section_sum(partial):
    count = lax.axis_size("section")
    if count != 2:
        return lax.psum(partial.astype(jnp.bfloat16), "section")
    mine = partial.astype(jnp.bfloat16)
    other = lax.ppermute(mine, "section", [(0, 1), (1, 0)])
    return (mine.astype(jnp.float32) + other.astype(jnp.float32)).astype(jnp.bfloat16)


def softmax_stats(scores, seen):
    row_top = jnp.max(jnp.where(seen, scores, -jnp.inf), axis=2, keepdims=True)
    raised = jnp.where(seen, jnp.exp(scores - row_top), 0.0)
    row_total = jnp.sum(raised, axis=2, keepdims=True)
    return raised / row_total, row_top, row_total


def per_device(normed, w_query, w_key, w_value, block_mask, cotangent):
    tokens = normed[0]
    upstream = cotangent[0]
    length = tokens.shape[0]
    features = upstream.shape[1]
    heads = features // HD
    blocks = length // BLOCK
    span_len = 2 * REACH + 1
    halo = REACH * BLOCK
    frame_blocks = blocks + 2 * REACH
    score_scale = HD ** (-0.5)

    left_tokens, right_tokens = neighbour_tokens(tokens, halo)
    left_up = shifted(upstream[length - halo :], "ctx", 1)
    right_up = shifted(upstream[:halo], "ctx", -1)
    gathered = lax.all_gather(jnp.stack([w_query, w_key, w_value]), "dp", axis=1, tiled=True)
    query_full, key_full, value_full = gathered[0], gathered[1], gathered[2]

    frame_tokens = jnp.concatenate([left_tokens, tokens, right_tokens], axis=0)
    all_weights = jnp.concatenate([query_full, key_full, value_full], axis=1)
    frame_proj = jnp.dot(frame_tokens, all_weights, preferred_element_type=jnp.float32).astype(
        jnp.bfloat16
    )
    query_h = head_major(frame_proj[:, :features], heads)
    key_h = head_major(frame_proj[:, features : 2 * features], heads)
    value_h = head_major(frame_proj[:, 2 * features :], heads)
    own_upstream = head_major(upstream, heads)
    near_upstream = head_major(jnp.concatenate([left_up, right_up], axis=0), heads)

    first_block = lax.axis_index("ctx") * blocks
    padded_mask = jnp.pad(block_mask, ((REACH, REACH), (0, 0)))
    frame_mask = lax.dynamic_slice(padded_mask, (first_block, 0), (frame_blocks, span_len))

    def rows(cells, at, count=1):
        return cells[:, at * BLOCK : (at + count) * BLOCK]

    def seen_keys(at, low, high):
        picked = frame_mask[at, low - at + REACH : high - at + REACH + 1] > 0
        return jnp.repeat(picked, BLOCK)[None, None, :]

    own_low, own_high = REACH, REACH + blocks - 1
    outs, query_grads, tops, totals, deltas = [], [], [], [], []
    own_score_grads, own_weights = [], []
    for i in range(blocks):
        at = REACH + i
        query_block = rows(query_h, at)
        upstream_block = rows(own_upstream, i)
        key_window = rows(key_h, i, span_len)
        value_window = rows(value_h, i, span_len)
        scores = (
            jnp.einsum("hqd,hkd->hqk", query_block, key_window, preferred_element_type=jnp.float32)
            * score_scale
        )
        probability, row_top, row_total = softmax_stats(scores, seen_keys(at, i, i + 2 * REACH))
        weights = probability.astype(jnp.bfloat16)
        outs.append(
            jnp.einsum("hqk,hkd->hqd", weights, value_window, preferred_element_type=jnp.float32)
        )
        prob_grad = jnp.einsum(
            "hqd,hkd->hqk", upstream_block, value_window, preferred_element_type=jnp.float32
        )
        row_delta = jnp.sum(probability * prob_grad, axis=2, keepdims=True)
        score_grad = (probability * (prob_grad - row_delta)).astype(jnp.bfloat16)
        query_grads.append(
            score_scale
            * jnp.einsum("hqk,hkd->hqd", score_grad, key_window, preferred_element_type=jnp.float32)
        )
        tops.append(row_top)
        totals.append(row_total)
        deltas.append(row_delta)
        cut = slice((own_low - i) * BLOCK, (own_high - i + 1) * BLOCK)
        own_score_grads.append(score_grad[:, :, cut])
        own_weights.append(weights[:, :, cut])

    attended = token_major(jnp.concatenate(outs, axis=1).astype(jnp.bfloat16))[None]
    query_grad = token_major(jnp.concatenate(query_grads, axis=1).astype(jnp.bfloat16))

    term_query = jnp.einsum(
        "tr,tf->rf", tokens, query_grad, preferred_element_type=jnp.float32
    ).astype(jnp.bfloat16)
    reduced_query = summed_rows(term_query)

    stats = jnp.stack(
        [jnp.concatenate(tops, axis=1), jnp.concatenate(totals, axis=1), jnp.concatenate(deltas, axis=1)]
    )
    stats_left = shifted(stats[:, :, length - halo :], "ctx", 1)
    stats_right = shifted(stats[:, :, :halo], "ctx", -1)

    near = list(range(REACH)) + list(range(REACH + blocks, frame_blocks))
    slots = np.arange(own_low, own_high + 1)[None, :] - np.array(near)[:, None] + REACH
    inside = (slots >= 0) & (slots < span_len)
    picked = frame_mask[np.array(near)[:, None], np.clip(slots, 0, span_len - 1)]
    allowed = (picked > 0) & inside
    allowed = jnp.repeat(jnp.repeat(allowed, BLOCK, axis=0), BLOCK, axis=1)[None]
    near_stats = jnp.concatenate([stats_left, stats_right], axis=2)
    top, total, delta = near_stats[0], near_stats[1], near_stats[2]
    near_query = jnp.concatenate([rows(query_h, 0, REACH), rows(query_h, REACH + blocks, REACH)], axis=1)
    key_part = rows(key_h, own_low, blocks)
    value_part = rows(value_h, own_low, blocks)
    scores = (
        jnp.einsum("hqd,hkd->hqk", near_query, key_part, preferred_element_type=jnp.float32)
        * score_scale
    )
    probability = jnp.where(allowed, jnp.exp(scores - top) / total, 0.0)
    weights = probability.astype(jnp.bfloat16)
    prob_grad = jnp.einsum(
        "hqd,hkd->hqk", near_upstream, value_part, preferred_element_type=jnp.float32
    )
    score_grad = (probability * (prob_grad - delta)).astype(jnp.bfloat16)
    all_score_grads = jnp.concatenate(own_score_grads + [score_grad], axis=1)
    every_weight = jnp.concatenate(own_weights + [weights], axis=1)
    all_queries = jnp.concatenate([rows(query_h, REACH, blocks), near_query], axis=1)
    all_upstream = jnp.concatenate([own_upstream, near_upstream], axis=1)
    key_own = score_scale * jnp.einsum(
        "hqk,hqd->hkd", all_score_grads, all_queries, preferred_element_type=jnp.float32
    )
    value_own = jnp.einsum(
        "hqk,hqd->hkd", every_weight, all_upstream, preferred_element_type=jnp.float32
    )

    key_grad = token_major(key_own).astype(jnp.bfloat16)
    value_grad = token_major(value_own).astype(jnp.bfloat16)

    contract = (((1,), (1,)), ((), ()))
    partial_input = lax.dot_general(
        jnp.concatenate([query_grad, key_grad, value_grad], axis=1),
        all_weights,
        contract,
        preferred_element_type=jnp.float32,
    )
    grad_input = section_sum(partial_input)[None]

    term_kv = jnp.einsum(
        "tr,tf->rf",
        tokens,
        jnp.concatenate([key_grad, value_grad], axis=1),
        preferred_element_type=jnp.float32,
    ).astype(jnp.bfloat16)
    reduced_kv = summed_rows(term_kv).reshape(-1, 2, features)
    summed = jnp.concatenate([reduced_query[:, None], reduced_kv], axis=1)
    grad_weights = summed / lax.axis_size("dp")
    return (attended, grad_input, grad_weights)


def solution(mesh):
    in_specs = (
        P("dp", "ctx", None),
        P("dp", "section"),
        P("dp", "section"),
        P("dp", "section"),
        P(),
        P("dp", "ctx", "section"),
    )
    out_specs = (P("dp", "ctx", "section"), P("dp", "ctx", None), P(("ctx", "dp"), None, "section"))
    return jax.shard_map(
        per_device, mesh=mesh, in_specs=in_specs, out_specs=out_specs, check_vma=False
    )
```

```python
import jax
import jax.numpy as jnp
import numpy as np
from jax import lax
from jax.sharding import PartitionSpec as P

HD = 64
BLOCK = 128
REACH = 3


def shifted(value, axis, steps):
    count = lax.axis_size(axis)
    leading, last = (max(0, -steps), min(count, count - steps))
    return lax.ppermute(value, axis, [(source, source + steps) for source in range(leading, last)])


def head_major(rows, heads):
    return rows.reshape(rows.shape[0], heads, HD).transpose(1, 0, 2)


def token_major(cells):
    return cells.transpose(1, 0, 2).reshape(cells.shape[1], cells.shape[0] * cells.shape[2])


def ordered_pair(mine, other, axis, dim):
    first = lax.axis_index(axis) == 0
    return jnp.where(
        first,
        jnp.concatenate([mine, other], axis=dim),
        jnp.concatenate([other, mine], axis=dim),
    )


def neighbour_tokens(tokens, halo):
    count = lax.axis_size("section")
    if count != 2:
        return (shifted(tokens[-halo:], "ctx", 1), shifted(tokens[:halo], "ctx", -1))
    half = tokens.shape[1] // 2
    start = lax.axis_index("section") * half
    share = lax.dynamic_slice_in_dim(tokens, start, half, 1)
    fetched = jnp.stack([shifted(share[-halo:], "ctx", 1), shifted(share[:halo], "ctx", -1)])
    partner = lax.ppermute(fetched, "section", [(0, 1), (1, 0)])
    both = ordered_pair(fetched, partner, "section", 2)
    return (both[0], both[1])


def full_rows(weight):
    if lax.axis_size("dp") != 2:
        return lax.all_gather(weight, "dp", axis=0, tiled=True)
    other = lax.ppermute(weight, "dp", [(0, 1), (1, 0)])
    return ordered_pair(weight, other, "dp", 0)


def summed_rows(term):
    group = ("ctx", "dp")
    count = lax.axis_size(group)
    parts = lax.all_to_all(term, group, 0, 0, tiled=True)
    parts = parts.reshape(count, term.shape[0] // count, *term.shape[1:])
    return jnp.sum(parts.astype(jnp.float32), axis=0)


def section_sum(partial):
    count = lax.axis_size("section")
    if count != 2:
        return lax.psum(partial.astype(jnp.bfloat16), "section")
    mine = partial.astype(jnp.bfloat16)
    other = lax.ppermute(mine, "section", [(0, 1), (1, 0)])
    return (mine.astype(jnp.float32) + other.astype(jnp.float32)).astype(jnp.bfloat16)


def softmax_stats(scores, seen):
    row_top = jnp.max(jnp.where(seen, scores, -jnp.inf), axis=2, keepdims=True)
    raised = jnp.where(seen, jnp.exp(scores - row_top), 0.0)
    row_total = jnp.sum(raised, axis=2, keepdims=True)
    return raised / row_total, row_top, row_total


def per_device(normed, w_query, w_key, w_value, block_mask, cotangent):
    tokens = normed[0]
    upstream = cotangent[0]
    length = tokens.shape[0]
    features = upstream.shape[1]
    heads = features // HD
    blocks = length // BLOCK
    span_len = 2 * REACH + 1
    halo = REACH * BLOCK
    frame_blocks = blocks + 2 * REACH
    score_scale = HD ** (-0.5)

    left_tokens, right_tokens = neighbour_tokens(tokens, halo)
    gathered = lax.all_gather(jnp.stack([w_query, w_key, w_value]), "dp", axis=1, tiled=True)
    query_full, key_full, value_full = gathered[0], gathered[1], gathered[2]

    frame_tokens = jnp.concatenate([left_tokens, tokens, right_tokens], axis=0)
    all_weights = jnp.concatenate([query_full, key_full, value_full], axis=1)
    frame_proj = jnp.dot(frame_tokens, all_weights, preferred_element_type=jnp.float32).astype(
        jnp.bfloat16
    )
    frame_proj, up_head, up_tail = lax.optimization_barrier(
        (frame_proj, upstream[:halo], upstream[length - halo :])
    )
    left_up = shifted(up_tail, "ctx", 1)
    right_up = shifted(up_head, "ctx", -1)
    query_h = head_major(frame_proj[:, :features], heads)
    key_h = head_major(frame_proj[:, features : 2 * features], heads)
    value_h = head_major(frame_proj[:, 2 * features :], heads)
    own_upstream = head_major(upstream, heads)
    near_upstream = head_major(jnp.concatenate([left_up, right_up], axis=0), heads)

    first_block = lax.axis_index("ctx") * blocks
    padded_mask = jnp.pad(block_mask, ((REACH, REACH), (0, 0)))
    frame_mask = lax.dynamic_slice(padded_mask, (first_block, 0), (frame_blocks, span_len))

    def rows(cells, at, count=1):
        return cells[:, at * BLOCK : (at + count) * BLOCK]

    def seen_keys(at, low, high):
        picked = frame_mask[at, low - at + REACH : high - at + REACH + 1] > 0
        return jnp.repeat(picked, BLOCK)[None, None, :]

    own_low, own_high = REACH, REACH + blocks - 1
    outs, query_grads, tops, totals, deltas = [], [], [], [], []
    own_score_grads, own_weights = [], []
    for i in range(blocks):
        at = REACH + i
        query_block = rows(query_h, at)
        upstream_block = rows(own_upstream, i)
        key_window = rows(key_h, i, span_len)
        value_window = rows(value_h, i, span_len)
        scores = (
            jnp.einsum("hqd,hkd->hqk", query_block, key_window, preferred_element_type=jnp.float32)
            * score_scale
        )
        probability, row_top, row_total = softmax_stats(scores, seen_keys(at, i, i + 2 * REACH))
        weights = probability.astype(jnp.bfloat16)
        outs.append(
            jnp.einsum("hqk,hkd->hqd", weights, value_window, preferred_element_type=jnp.float32)
        )
        prob_grad = jnp.einsum(
            "hqd,hkd->hqk", upstream_block, value_window, preferred_element_type=jnp.float32
        )
        row_delta = jnp.sum(probability * prob_grad, axis=2, keepdims=True)
        score_grad = (probability * (prob_grad - row_delta)).astype(jnp.bfloat16)
        query_grads.append(
            score_scale
            * jnp.einsum("hqk,hkd->hqd", score_grad, key_window, preferred_element_type=jnp.float32)
        )
        tops.append(row_top)
        totals.append(row_total)
        deltas.append(row_delta)
        cut = slice((own_low - i) * BLOCK, (own_high - i + 1) * BLOCK)
        own_score_grads.append(score_grad[:, :, cut])
        own_weights.append(weights[:, :, cut])

    attended = token_major(jnp.concatenate(outs, axis=1).astype(jnp.bfloat16))[None]
    query_grad = token_major(jnp.concatenate(query_grads, axis=1).astype(jnp.bfloat16))

    term_query = jnp.einsum(
        "tr,tf->rf", tokens, query_grad, preferred_element_type=jnp.float32
    ).astype(jnp.bfloat16)
    reduced_query = summed_rows(term_query)

    stats = jnp.stack(
        [jnp.concatenate(tops, axis=1), jnp.concatenate(totals, axis=1), jnp.concatenate(deltas, axis=1)]
    )
    stats_left = shifted(stats[:, :, length - halo :], "ctx", 1)
    stats_right = shifted(stats[:, :, :halo], "ctx", -1)

    near = list(range(REACH)) + list(range(REACH + blocks, frame_blocks))
    slots = np.arange(own_low, own_high + 1)[None, :] - np.array(near)[:, None] + REACH
    inside = (slots >= 0) & (slots < span_len)
    picked = frame_mask[np.array(near)[:, None], np.clip(slots, 0, span_len - 1)]
    allowed = (picked > 0) & inside
    allowed = jnp.repeat(jnp.repeat(allowed, BLOCK, axis=0), BLOCK, axis=1)[None]
    near_stats = jnp.concatenate([stats_left, stats_right], axis=2)
    top, total, delta = near_stats[0], near_stats[1], near_stats[2]
    near_query = jnp.concatenate([rows(query_h, 0, REACH), rows(query_h, REACH + blocks, REACH)], axis=1)
    key_part = rows(key_h, own_low, blocks)
    value_part = rows(value_h, own_low, blocks)
    scores = (
        jnp.einsum("hqd,hkd->hqk", near_query, key_part, preferred_element_type=jnp.float32)
        * score_scale
    )
    probability = jnp.where(allowed, jnp.exp(scores - top) / total, 0.0)
    weights = probability.astype(jnp.bfloat16)
    prob_grad = jnp.einsum(
        "hqd,hkd->hqk", near_upstream, value_part, preferred_element_type=jnp.float32
    )
    score_grad = (probability * (prob_grad - delta)).astype(jnp.bfloat16)
    all_score_grads = jnp.concatenate(own_score_grads + [score_grad], axis=1)
    every_weight = jnp.concatenate(own_weights + [weights], axis=1)
    all_queries = jnp.concatenate([rows(query_h, REACH, blocks), near_query], axis=1)
    all_upstream = jnp.concatenate([own_upstream, near_upstream], axis=1)
    key_own = score_scale * jnp.einsum(
        "hqk,hqd->hkd", all_score_grads, all_queries, preferred_element_type=jnp.float32
    )
    value_own = jnp.einsum(
        "hqk,hqd->hkd", every_weight, all_upstream, preferred_element_type=jnp.float32
    )

    key_grad = token_major(key_own).astype(jnp.bfloat16)
    value_grad = token_major(value_own).astype(jnp.bfloat16)

    contract = (((1,), (1,)), ((), ()))
    partial_input = lax.dot_general(
        jnp.concatenate([query_grad, key_grad, value_grad], axis=1),
        all_weights,
        contract,
        preferred_element_type=jnp.float32,
    )
    grad_input = section_sum(partial_input)[None]

    term_kv = jnp.einsum(
        "tr,tf->rf",
        tokens,
        jnp.concatenate([key_grad, value_grad], axis=1),
        preferred_element_type=jnp.float32,
    ).astype(jnp.bfloat16)
    reduced_kv = summed_rows(term_kv).reshape(-1, 2, features)
    summed = jnp.concatenate([reduced_query[:, None], reduced_kv], axis=1)
    grad_weights = summed / lax.axis_size("dp")
    return (attended, grad_input, grad_weights)


def solution(mesh):
    in_specs = (
        P("dp", "ctx", None),
        P("dp", "section"),
        P("dp", "section"),
        P("dp", "section"),
        P(),
        P("dp", "ctx", "section"),
    )
    out_specs = (P("dp", "ctx", "section"), P("dp", "ctx", None), P(("ctx", "dp"), None, "section"))
    return jax.shard_map(
        per_device, mesh=mesh, in_specs=in_specs, out_specs=out_specs, check_vma=False
    )
```

```python
import jax
import jax.numpy as jnp
import numpy as np
from jax import lax
from jax.sharding import PartitionSpec as P

HD = 64
BLOCK = 128
REACH = 3


def shifted(value, axis, steps):
    count = lax.axis_size(axis)
    leading, last = (max(0, -steps), min(count, count - steps))
    return lax.ppermute(value, axis, [(source, source + steps) for source in range(leading, last)])


def head_major(rows, heads):
    return rows.reshape(rows.shape[0], heads, HD).transpose(1, 0, 2)


def token_major(cells):
    return cells.transpose(1, 0, 2).reshape(cells.shape[1], cells.shape[0] * cells.shape[2])


def ordered_pair(mine, other, axis, dim):
    first = lax.axis_index(axis) == 0
    return jnp.where(
        first,
        jnp.concatenate([mine, other], axis=dim),
        jnp.concatenate([other, mine], axis=dim),
    )


def neighbour_tokens(tokens, halo):
    count = lax.axis_size("section")
    if count != 2:
        return (shifted(tokens[-halo:], "ctx", 1), shifted(tokens[:halo], "ctx", -1))
    half = tokens.shape[1] // 2
    start = lax.axis_index("section") * half
    share = lax.dynamic_slice_in_dim(tokens, start, half, 1)
    fetched = jnp.stack([shifted(share[-halo:], "ctx", 1), shifted(share[:halo], "ctx", -1)])
    partner = lax.ppermute(fetched, "section", [(0, 1), (1, 0)])
    both = ordered_pair(fetched, partner, "section", 2)
    return (both[0], both[1])


def full_rows(weight):
    if lax.axis_size("dp") != 2:
        return lax.all_gather(weight, "dp", axis=0, tiled=True)
    other = lax.ppermute(weight, "dp", [(0, 1), (1, 0)])
    return ordered_pair(weight, other, "dp", 0)


def summed_rows(term):
    group = ("ctx", "dp")
    count = lax.axis_size(group)
    parts = lax.all_to_all(term, group, 0, 0, tiled=True)
    parts = parts.reshape(count, term.shape[0] // count, *term.shape[1:])
    return jnp.sum(parts.astype(jnp.float32), axis=0)


def section_sum(partial):
    count = lax.axis_size("section")
    if count != 2:
        return lax.psum(partial.astype(jnp.bfloat16), "section")
    mine = partial.astype(jnp.bfloat16)
    other = lax.ppermute(mine, "section", [(0, 1), (1, 0)])
    return (mine.astype(jnp.float32) + other.astype(jnp.float32)).astype(jnp.bfloat16)


def softmax_stats(scores, seen):
    row_top = jnp.max(jnp.where(seen, scores, -jnp.inf), axis=2, keepdims=True)
    raised = jnp.where(seen, jnp.exp(scores - row_top), 0.0)
    row_total = jnp.sum(raised, axis=2, keepdims=True)
    return raised / row_total, row_top, row_total


def per_device(normed, w_query, w_key, w_value, block_mask, cotangent):
    tokens = normed[0]
    upstream = cotangent[0]
    length = tokens.shape[0]
    features = upstream.shape[1]
    heads = features // HD
    blocks = length // BLOCK
    span_len = 2 * REACH + 1
    halo = REACH * BLOCK
    frame_blocks = blocks + 2 * REACH
    score_scale = HD ** (-0.5)

    left_tokens, right_tokens = neighbour_tokens(tokens, halo)
    left_up = shifted(upstream[length - halo :], "ctx", 1)
    right_up = shifted(upstream[:halo], "ctx", -1)
    gathered = lax.all_gather(jnp.stack([w_query, w_key, w_value]), "dp", axis=1, tiled=True)
    query_full, key_full, value_full = gathered[0], gathered[1], gathered[2]

    frame_tokens = jnp.concatenate([left_tokens, tokens, right_tokens], axis=0)
    all_weights = jnp.concatenate([query_full, key_full, value_full], axis=1)
    if lax.axis_size("dp") == 2:
        share = w_query.shape[0]
        mine = lax.axis_index("dp") * share
        local_weights = jnp.concatenate([w_query, w_key, w_value], axis=1)
        remote_weights = lax.dynamic_slice_in_dim(all_weights, share - mine, share, 0)
        local_part = jnp.dot(
            lax.dynamic_slice_in_dim(frame_tokens, mine, share, 1),
            local_weights,
            preferred_element_type=jnp.float32,
        )
        remote_part = jnp.dot(
            lax.dynamic_slice_in_dim(frame_tokens, share - mine, share, 1),
            remote_weights,
            preferred_element_type=jnp.float32,
        )
        frame_proj = (local_part + remote_part).astype(jnp.bfloat16)
    else:
        frame_proj = jnp.dot(
            frame_tokens, all_weights, preferred_element_type=jnp.float32
        ).astype(jnp.bfloat16)
    query_h = head_major(frame_proj[:, :features], heads)
    key_h = head_major(frame_proj[:, features : 2 * features], heads)
    value_h = head_major(frame_proj[:, 2 * features :], heads)
    own_upstream = head_major(upstream, heads)
    near_upstream = head_major(jnp.concatenate([left_up, right_up], axis=0), heads)

    first_block = lax.axis_index("ctx") * blocks
    padded_mask = jnp.pad(block_mask, ((REACH, REACH), (0, 0)))
    frame_mask = lax.dynamic_slice(padded_mask, (first_block, 0), (frame_blocks, span_len))

    def rows(cells, at, count=1):
        return cells[:, at * BLOCK : (at + count) * BLOCK]

    def seen_keys(at, low, high):
        picked = frame_mask[at, low - at + REACH : high - at + REACH + 1] > 0
        return jnp.repeat(picked, BLOCK)[None, None, :]

    own_low, own_high = REACH, REACH + blocks - 1
    outs, query_grads, tops, totals, deltas = [], [], [], [], []
    own_score_grads, own_weights = [], []
    for i in range(blocks):
        at = REACH + i
        query_block = rows(query_h, at)
        upstream_block = rows(own_upstream, i)
        key_window = rows(key_h, i, span_len)
        value_window = rows(value_h, i, span_len)
        scores = (
            jnp.einsum("hqd,hkd->hqk", query_block, key_window, preferred_element_type=jnp.float32)
            * score_scale
        )
        probability, row_top, row_total = softmax_stats(scores, seen_keys(at, i, i + 2 * REACH))
        weights = probability.astype(jnp.bfloat16)
        outs.append(
            jnp.einsum("hqk,hkd->hqd", weights, value_window, preferred_element_type=jnp.float32)
        )
        prob_grad = jnp.einsum(
            "hqd,hkd->hqk", upstream_block, value_window, preferred_element_type=jnp.float32
        )
        row_delta = jnp.sum(probability * prob_grad, axis=2, keepdims=True)
        score_grad = (probability * (prob_grad - row_delta)).astype(jnp.bfloat16)
        query_grads.append(
            score_scale
            * jnp.einsum("hqk,hkd->hqd", score_grad, key_window, preferred_element_type=jnp.float32)
        )
        tops.append(row_top)
        totals.append(row_total)
        deltas.append(row_delta)
        cut = slice((own_low - i) * BLOCK, (own_high - i + 1) * BLOCK)
        own_score_grads.append(score_grad[:, :, cut])
        own_weights.append(weights[:, :, cut])

    attended = token_major(jnp.concatenate(outs, axis=1).astype(jnp.bfloat16))[None]
    query_grad = token_major(jnp.concatenate(query_grads, axis=1).astype(jnp.bfloat16))

    term_query = jnp.einsum(
        "tr,tf->rf", tokens, query_grad, preferred_element_type=jnp.float32
    ).astype(jnp.bfloat16)
    reduced_query = summed_rows(term_query)

    stats = jnp.stack(
        [jnp.concatenate(tops, axis=1), jnp.concatenate(totals, axis=1), jnp.concatenate(deltas, axis=1)]
    )
    stats_left = shifted(stats[:, :, length - halo :], "ctx", 1)
    stats_right = shifted(stats[:, :, :halo], "ctx", -1)

    near = list(range(REACH)) + list(range(REACH + blocks, frame_blocks))
    slots = np.arange(own_low, own_high + 1)[None, :] - np.array(near)[:, None] + REACH
    inside = (slots >= 0) & (slots < span_len)
    picked = frame_mask[np.array(near)[:, None], np.clip(slots, 0, span_len - 1)]
    allowed = (picked > 0) & inside
    allowed = jnp.repeat(jnp.repeat(allowed, BLOCK, axis=0), BLOCK, axis=1)[None]
    near_stats = jnp.concatenate([stats_left, stats_right], axis=2)
    top, total, delta = near_stats[0], near_stats[1], near_stats[2]
    near_query = jnp.concatenate([rows(query_h, 0, REACH), rows(query_h, REACH + blocks, REACH)], axis=1)
    key_part = rows(key_h, own_low, blocks)
    value_part = rows(value_h, own_low, blocks)
    scores = (
        jnp.einsum("hqd,hkd->hqk", near_query, key_part, preferred_element_type=jnp.float32)
        * score_scale
    )
    probability = jnp.where(allowed, jnp.exp(scores - top) / total, 0.0)
    weights = probability.astype(jnp.bfloat16)
    prob_grad = jnp.einsum(
        "hqd,hkd->hqk", near_upstream, value_part, preferred_element_type=jnp.float32
    )
    score_grad = (probability * (prob_grad - delta)).astype(jnp.bfloat16)
    all_score_grads = jnp.concatenate(own_score_grads + [score_grad], axis=1)
    every_weight = jnp.concatenate(own_weights + [weights], axis=1)
    all_queries = jnp.concatenate([rows(query_h, REACH, blocks), near_query], axis=1)
    all_upstream = jnp.concatenate([own_upstream, near_upstream], axis=1)
    key_own = score_scale * jnp.einsum(
        "hqk,hqd->hkd", all_score_grads, all_queries, preferred_element_type=jnp.float32
    )
    value_own = jnp.einsum(
        "hqk,hqd->hkd", every_weight, all_upstream, preferred_element_type=jnp.float32
    )

    key_grad = token_major(key_own).astype(jnp.bfloat16)
    value_grad = token_major(value_own).astype(jnp.bfloat16)

    contract = (((1,), (1,)), ((), ()))
    partial_input = lax.dot_general(
        jnp.concatenate([query_grad, key_grad, value_grad], axis=1),
        all_weights,
        contract,
        preferred_element_type=jnp.float32,
    )
    grad_input = section_sum(partial_input)[None]

    term_kv = jnp.einsum(
        "tr,tf->rf",
        tokens,
        jnp.concatenate([key_grad, value_grad], axis=1),
        preferred_element_type=jnp.float32,
    ).astype(jnp.bfloat16)
    reduced_kv = summed_rows(term_kv).reshape(-1, 2, features)
    summed = jnp.concatenate([reduced_query[:, None], reduced_kv], axis=1)
    grad_weights = summed / lax.axis_size("dp")
    return (attended, grad_input, grad_weights)


def solution(mesh):
    in_specs = (
        P("dp", "ctx", None),
        P("dp", "section"),
        P("dp", "section"),
        P("dp", "section"),
        P(),
        P("dp", "ctx", "section"),
    )
    out_specs = (P("dp", "ctx", "section"), P("dp", "ctx", None), P(("ctx", "dp"), None, "section"))
    return jax.shard_map(
        per_device, mesh=mesh, in_specs=in_specs, out_specs=out_specs, check_vma=False
    )
```

```python
import jax
import jax.numpy as jnp
import numpy as np
from jax import lax
from jax.sharding import PartitionSpec as P

HD = 64
BLOCK = 128
REACH = 3


def shifted(value, axis, steps):
    count = lax.axis_size(axis)
    leading, last = (max(0, -steps), min(count, count - steps))
    return lax.ppermute(value, axis, [(source, source + steps) for source in range(leading, last)])


def head_major(rows, heads):
    return rows.reshape(rows.shape[0], heads, HD).transpose(1, 0, 2)


def token_major(cells):
    return cells.transpose(1, 0, 2).reshape(cells.shape[1], cells.shape[0] * cells.shape[2])


def ordered_pair(mine, other, axis, dim):
    first = lax.axis_index(axis) == 0
    return jnp.where(
        first,
        jnp.concatenate([mine, other], axis=dim),
        jnp.concatenate([other, mine], axis=dim),
    )


def neighbour_tokens(tokens, halo):
    count = lax.axis_size("section")
    if count != 2:
        return (shifted(tokens[-halo:], "ctx", 1), shifted(tokens[:halo], "ctx", -1))
    half = tokens.shape[1] // 2
    start = lax.axis_index("section") * half
    share = lax.dynamic_slice_in_dim(tokens, start, half, 1)
    fetched = jnp.stack([shifted(share[-halo:], "ctx", 1), shifted(share[:halo], "ctx", -1)])
    partner = lax.ppermute(fetched, "section", [(0, 1), (1, 0)])
    both = ordered_pair(fetched, partner, "section", 2)
    return (both[0], both[1])


def full_rows(weight):
    if lax.axis_size("dp") != 2:
        return lax.all_gather(weight, "dp", axis=0, tiled=True)
    other = lax.ppermute(weight, "dp", [(0, 1), (1, 0)])
    return ordered_pair(weight, other, "dp", 0)


def summed_rows(term):
    group = ("ctx", "dp")
    count = lax.axis_size(group)
    parts = lax.all_to_all(term, group, 0, 0, tiled=True)
    parts = parts.reshape(count, term.shape[0] // count, *term.shape[1:])
    return jnp.sum(parts.astype(jnp.float32), axis=0)


def section_sum(partial):
    count = lax.axis_size("section")
    if count != 2:
        return lax.psum(partial.astype(jnp.bfloat16), "section")
    mine = partial.astype(jnp.bfloat16)
    other = lax.ppermute(mine, "section", [(0, 1), (1, 0)])
    return (mine.astype(jnp.float32) + other.astype(jnp.float32)).astype(jnp.bfloat16)


def softmax_stats(scores, seen):
    row_top = jnp.max(jnp.where(seen, scores, -jnp.inf), axis=2, keepdims=True)
    raised = jnp.where(seen, jnp.exp(scores - row_top), 0.0)
    row_total = jnp.sum(raised, axis=2, keepdims=True)
    return raised / row_total, row_top, row_total


def per_device(normed, w_query, w_key, w_value, block_mask, cotangent):
    tokens = normed[0]
    upstream = cotangent[0]
    length = tokens.shape[0]
    features = upstream.shape[1]
    heads = features // HD
    blocks = length // BLOCK
    span_len = 2 * REACH + 1
    halo = REACH * BLOCK
    frame_blocks = blocks + 2 * REACH
    score_scale = HD ** (-0.5)

    left_tokens, right_tokens = neighbour_tokens(tokens, halo)
    left_up = shifted(upstream[length - halo :], "ctx", 1)
    right_up = shifted(upstream[:halo], "ctx", -1)
    query_full = full_rows(w_query)
    gathered = lax.all_gather(jnp.stack([w_key, w_value]), "dp", axis=1, tiled=True)
    key_full, value_full = gathered[0], gathered[1]

    frame_tokens = jnp.concatenate([left_tokens, tokens, right_tokens], axis=0)
    all_weights = jnp.concatenate([query_full, key_full, value_full], axis=1)
    frame_proj = jnp.dot(frame_tokens, all_weights, preferred_element_type=jnp.float32).astype(
        jnp.bfloat16
    )
    query_h = head_major(frame_proj[:, :features], heads)
    key_h = head_major(frame_proj[:, features : 2 * features], heads)
    value_h = head_major(frame_proj[:, 2 * features :], heads)
    own_upstream = head_major(upstream, heads)
    near_upstream = head_major(jnp.concatenate([left_up, right_up], axis=0), heads)

    first_block = lax.axis_index("ctx") * blocks
    padded_mask = jnp.pad(block_mask, ((REACH, REACH), (0, 0)))
    frame_mask = lax.dynamic_slice(padded_mask, (first_block, 0), (frame_blocks, span_len))

    def rows(cells, at, count=1):
        return cells[:, at * BLOCK : (at + count) * BLOCK]

    def seen_keys(at, low, high):
        picked = frame_mask[at, low - at + REACH : high - at + REACH + 1] > 0
        return jnp.repeat(picked, BLOCK)[None, None, :]

    own_low, own_high = REACH, REACH + blocks - 1
    outs, query_grads, tops, totals, deltas = [], [], [], [], []
    own_score_grads, own_weights = [], []
    for i in range(blocks):
        at = REACH + i
        query_block = rows(query_h, at)
        upstream_block = rows(own_upstream, i)
        key_window = rows(key_h, i, span_len)
        value_window = rows(value_h, i, span_len)
        scores = (
            jnp.einsum("hqd,hkd->hqk", query_block, key_window, preferred_element_type=jnp.float32)
            * score_scale
        )
        probability, row_top, row_total = softmax_stats(scores, seen_keys(at, i, i + 2 * REACH))
        weights = probability.astype(jnp.bfloat16)
        outs.append(
            jnp.einsum("hqk,hkd->hqd", weights, value_window, preferred_element_type=jnp.float32)
        )
        prob_grad = jnp.einsum(
            "hqd,hkd->hqk", upstream_block, value_window, preferred_element_type=jnp.float32
        )
        row_delta = jnp.sum(probability * prob_grad, axis=2, keepdims=True)
        score_grad = (probability * (prob_grad - row_delta)).astype(jnp.bfloat16)
        query_grads.append(
            score_scale
            * jnp.einsum("hqk,hkd->hqd", score_grad, key_window, preferred_element_type=jnp.float32)
        )
        tops.append(row_top)
        totals.append(row_total)
        deltas.append(row_delta)
        cut = slice((own_low - i) * BLOCK, (own_high - i + 1) * BLOCK)
        own_score_grads.append(score_grad[:, :, cut])
        own_weights.append(weights[:, :, cut])

    attended = token_major(jnp.concatenate(outs, axis=1).astype(jnp.bfloat16))[None]
    query_grad = token_major(jnp.concatenate(query_grads, axis=1).astype(jnp.bfloat16))

    term_query = jnp.einsum(
        "tr,tf->rf", tokens, query_grad, preferred_element_type=jnp.float32
    ).astype(jnp.bfloat16)
    reduced_query = summed_rows(term_query)

    stats = jnp.stack(
        [jnp.concatenate(tops, axis=1), jnp.concatenate(totals, axis=1), jnp.concatenate(deltas, axis=1)]
    )
    stats_left = shifted(stats[:, :, length - halo :], "ctx", 1)
    stats_right = shifted(stats[:, :, :halo], "ctx", -1)

    near = list(range(REACH)) + list(range(REACH + blocks, frame_blocks))
    slots = np.arange(own_low, own_high + 1)[None, :] - np.array(near)[:, None] + REACH
    inside = (slots >= 0) & (slots < span_len)
    picked = frame_mask[np.array(near)[:, None], np.clip(slots, 0, span_len - 1)]
    allowed = (picked > 0) & inside
    allowed = jnp.repeat(jnp.repeat(allowed, BLOCK, axis=0), BLOCK, axis=1)[None]
    near_stats = jnp.concatenate([stats_left, stats_right], axis=2)
    top, total, delta = near_stats[0], near_stats[1], near_stats[2]
    near_query = jnp.concatenate([rows(query_h, 0, REACH), rows(query_h, REACH + blocks, REACH)], axis=1)
    key_part = rows(key_h, own_low, blocks)
    value_part = rows(value_h, own_low, blocks)
    scores = (
        jnp.einsum("hqd,hkd->hqk", near_query, key_part, preferred_element_type=jnp.float32)
        * score_scale
    )
    probability = jnp.where(allowed, jnp.exp(scores - top) / total, 0.0)
    weights = probability.astype(jnp.bfloat16)
    prob_grad = jnp.einsum(
        "hqd,hkd->hqk", near_upstream, value_part, preferred_element_type=jnp.float32
    )
    score_grad = (probability * (prob_grad - delta)).astype(jnp.bfloat16)
    all_score_grads = jnp.concatenate(own_score_grads + [score_grad], axis=1)
    every_weight = jnp.concatenate(own_weights + [weights], axis=1)
    all_queries = jnp.concatenate([rows(query_h, REACH, blocks), near_query], axis=1)
    all_upstream = jnp.concatenate([own_upstream, near_upstream], axis=1)
    key_own = score_scale * jnp.einsum(
        "hqk,hqd->hkd", all_score_grads, all_queries, preferred_element_type=jnp.float32
    )
    value_own = jnp.einsum(
        "hqk,hqd->hkd", every_weight, all_upstream, preferred_element_type=jnp.float32
    )

    key_grad = token_major(key_own).astype(jnp.bfloat16)
    value_grad = token_major(value_own).astype(jnp.bfloat16)

    contract = (((1,), (1,)), ((), ()))
    partial_input = lax.dot_general(
        jnp.concatenate([query_grad, key_grad, value_grad], axis=1),
        all_weights,
        contract,
        preferred_element_type=jnp.float32,
    )
    grad_input = section_sum(partial_input)[None]

    term_kv = jnp.einsum(
        "tr,tf->rf",
        tokens,
        jnp.concatenate([key_grad, value_grad], axis=1),
        preferred_element_type=jnp.float32,
    ).astype(jnp.bfloat16)
    reduced_kv = summed_rows(term_kv).reshape(-1, 2, features)
    summed = jnp.concatenate([reduced_query[:, None], reduced_kv], axis=1)
    grad_weights = summed / lax.axis_size("dp")
    return (attended, grad_input, grad_weights)


def solution(mesh):
    in_specs = (
        P("dp", "ctx", None),
        P("dp", "section"),
        P("dp", "section"),
        P("dp", "section"),
        P(),
        P("dp", "ctx", "section"),
    )
    out_specs = (P("dp", "ctx", "section"), P("dp", "ctx", None), P(("ctx", "dp"), None, "section"))
    return jax.shard_map(
        per_device, mesh=mesh, in_specs=in_specs, out_specs=out_specs, check_vma=False
    )
```
